256 devices in a mesh: dp: 32 (over z, x), seq: 8 (over y, core).
Axes of the slice: x: 4, y: 4, z: 8, core: 2. Of those that a mesh axis runs over, the one named last changes fastest.
Arguments:
- hidden: bfloat16 [32, 6144, 2560], P('dp', 'seq'), may hold values from -6 to 6
- log_decay: float32 [32, 40, 6144], P('dp', None, 'seq'), may hold values from -2 to 0, as said below
- input_weight: bfloat16 [2816, 2560], P(('dp', 'seq')), may hold values from -0.125 to 0.125
- conv_weight: bfloat16 [4, 2816], replicated, may hold values from -3 to 3
- conv_bias: float32 [2816], replicated, may hold values from -0.5 to 0.5
- skip_gain: float32 [40], replicated, may hold values from 0.5 to 1.5
Outputs:
- mixer_out: bfloat16 [32, 6144, 2560], P('dp', 'seq')
The draws below stay inside these ranges and needn't reach their ends.
Inputs may be any that keep to these rules, and one draw needn't show every extreme that they name: `log_decay`: every value is negative.
All inputs are finite; a program needn't handle non-finite values.
Results may differ from the reference program's by a relative error of at most 0.0064.
Values may be sent and summed in bfloat16 or wider, within the bound.
No kernel may reach another device: no remote copies, remote signals or barrier semaphores. Data moves between devices by JAX's collectives and lax.ppermute only.
A program may use at most 128 MiB of HBM per device.

```python
import math
import jax
import jax.numpy as jnp
from jax import lax

D = 2560
HALF_HEADS = 40
HEAD_DIM = 64
STATE = 128
SPAN = 256
CONV = 4
TOK_DEV = 768
INNER = 2560
COLS = 2816
BATCH_CONTEXTS = 32
CONTEXT_LENGTH = 6144


def draw_log_decay(key, part):
    random_keys = jax.random.split(key, 7)
    fast_share = 0.5
    blocks = CONTEXT_LENGTH // TOK_DEV
    fast = (jax.random.uniform(random_keys[0], (BATCH_CONTEXTS, HALF_HEADS, 1)) < fast_share).astype(jnp.float32)
    slow_rate = jax.random.uniform(random_keys[1], (BATCH_CONTEXTS, HALF_HEADS, 1), minval=0.3, maxval=0.9) / CONTEXT_LENGTH
    fast_rate = jax.random.uniform(random_keys[2], (BATCH_CONTEXTS, HALF_HEADS, 1), minval=5.0, maxval=8.0) / SPAN
    baseline_rate = fast * fast_rate + (1.0 - fast) * slow_rate
    shard_multiplier = jnp.exp(jax.random.uniform(random_keys[3], (BATCH_CONTEXTS, HALF_HEADS, blocks, 1), minval=math.log(0.5), maxval=math.log(1.5)))
    shard_multiplier = jnp.broadcast_to(shard_multiplier, (BATCH_CONTEXTS, HALF_HEADS, blocks, TOK_DEV)).reshape(BATCH_CONTEXTS, HALF_HEADS, CONTEXT_LENGTH)
    jitter_level = jax.random.uniform(random_keys[4], (BATCH_CONTEXTS, HALF_HEADS, CONTEXT_LENGTH), minval=0.6, maxval=1.4)
    spike_position = jax.random.randint(random_keys[5], (BATCH_CONTEXTS, 4, 1), 0, CONTEXT_LENGTH)
    spike_strength = jnp.any(jnp.arange(CONTEXT_LENGTH)[None, None, :] == spike_position, axis=1, keepdims=True).astype(jnp.float32)
    spike_falloff = jax.random.uniform(random_keys[6], (BATCH_CONTEXTS, HALF_HEADS, 1), minval=0.22, maxval=0.69)
    return -(baseline_rate * shard_multiplier * jitter_level + spike_strength * spike_falloff)


def block_scale(own_key, extent, cuts, smallest, largest):
    def one(axis_at, parts):
        draws = jax.random.uniform(jax.random.fold_in(jax.random.fold_in(own_key, 6), axis_at), (parts,), jnp.float32, smallest / len(cuts), largest / len(cuts))
        return jnp.repeat(jnp.exp(draws), extent[axis_at] // parts).reshape((-1,) + (1,) * (len(extent) - axis_at - 1))

    level = one(*cuts[0])
    for cut in cuts[1:]:
        level = level * one(*cut)
    return level


def centred(key, dims, width, reach, cuts=(), dtype=jnp.bfloat16):
    loudness = block_scale(key, dims, cuts, -0.22, 0.18) if cuts else 1.0
    drawn = jax.random.normal(key, dims, jnp.float32) * width * loudness
    return jnp.minimum(jnp.maximum(drawn, -reach), reach).astype(dtype)


def setup_inputs(seed: int = 0) -> dict:
    arg_keys = jax.random.split(jax.random.key(seed), 7)
    hidden = centred(arg_keys[0], (BATCH_CONTEXTS, CONTEXT_LENGTH, D), 1.0, 6.0, ((0, 32), (1, 8)))
    log_decay = draw_log_decay(jax.random.fold_in(arg_keys[6], 71), 0)
    input_weight = centred(arg_keys[2], (COLS, D), D ** -0.5, 0.125, ((0, 256),))
    conv_weight = centred(arg_keys[3], (CONV, COLS), CONV ** -0.5, 3.0)
    conv_bias = jnp.clip(jax.random.uniform(arg_keys[4], (COLS,), jnp.float32, -0.5, 0.5), -0.5, 0.5)
    skip_gain = jnp.clip(jax.random.uniform(arg_keys[5], (HALF_HEADS,), jnp.float32, 0.5, 1.5), 0.5, 1.5)
    return dict(hidden=hidden, log_decay=log_decay, input_weight=input_weight, conv_weight=conv_weight, conv_bias=conv_bias, skip_gain=skip_gain)


def mixing_output(x_heads, b_span, c_span, cumulative, step_size):
    scores = jnp.dot(c_span, b_span.T, preferred_element_type=jnp.float32)
    span_len = cumulative.shape[1]
    causal = jnp.arange(span_len)[:, None] >= jnp.arange(span_len)[None, :]
    spread = jnp.where(causal[None], cumulative[:, :, None] - cumulative[:, None, :], -jnp.inf)
    mixing = (scores[None] * jnp.exp(spread) * step_size[:, None, :]).astype(jnp.bfloat16)
    return jnp.einsum("hqk,khp->qhp", mixing.astype(jnp.float32), x_heads.astype(jnp.float32))


def span_state(x_heads, b_span, cumulative, step_size):
    weight = jnp.exp(cumulative[:, -1:] - cumulative) * step_size
    decayed = (x_heads * weight.T[:, :, None]).astype(jnp.bfloat16)
    return jnp.einsum("khp,kn->hpn", decayed.astype(jnp.float32), b_span.astype(jnp.float32))


def state_output(c_span, entering, cumulative):
    readout = jnp.einsum("qn,hpn->qhp", c_span.astype(jnp.float32), entering, precision=lax.Precision.HIGHEST)
    return jnp.exp(cumulative).T[:, :, None] * readout


def reference(hidden, log_decay, input_weight, conv_weight, conv_bias, skip_gain):
    def one_context(operands):
        token_rows, decay_rows = operands
        projected = lax.dot_general(token_rows, input_weight, (((1,), (1,)), ((), ())), preferred_element_type=jnp.float32).astype(jnp.bfloat16)
        padded = jnp.concatenate([jnp.zeros((CONV - 1, COLS), jnp.bfloat16), projected], axis=0)
        filtered = jnp.broadcast_to(conv_bias[None, :], (CONTEXT_LENGTH, COLS))
        for kernel_tap in range(CONV):
            filtered = filtered + padded[kernel_tap:kernel_tap + CONTEXT_LENGTH].astype(jnp.float32) * conv_weight[kernel_tap].astype(jnp.float32)[None, :]
        active = jax.nn.silu(filtered).astype(jnp.bfloat16)
        span_count = CONTEXT_LENGTH // SPAN
        x_all = active[:, :INNER].reshape(span_count, SPAN, HALF_HEADS, HEAD_DIM)
        b_all = active[:, INNER:INNER + STATE].reshape(span_count, SPAN, STATE)
        c_all = active[:, INNER + STATE:].reshape(span_count, SPAN, STATE)
        decay_spans = decay_rows.reshape(HALF_HEADS, span_count, SPAN).transpose(1, 0, 2)
        cumulative = jnp.cumsum(decay_spans, axis=2)

        def advance(entering, inputs):
            x_heads, b_span, c_span, cum_span, decay_span = inputs
            step_size = -decay_span
            outputs = mixing_output(x_heads, b_span, c_span, cum_span, step_size) + state_output(c_span, entering, cum_span)
            new_state = jnp.exp(cum_span[:, -1])[:, None, None] * entering + span_state(x_heads, b_span, cum_span, step_size)
            return new_state, outputs

        start_state = jnp.zeros((HALF_HEADS, HEAD_DIM, STATE), jnp.float32)
        _, outputs = lax.scan(advance, start_state, (x_all, b_all, c_all, cumulative, decay_spans))
        outputs = outputs.reshape(CONTEXT_LENGTH, HALF_HEADS, HEAD_DIM) + skip_gain[None, :, None] * x_all.reshape(CONTEXT_LENGTH, HALF_HEADS, HEAD_DIM).astype(jnp.float32)
        return outputs.reshape(CONTEXT_LENGTH, INNER).astype(jnp.bfloat16)

    return lax.map(one_context, (hidden, log_decay))
```

```python
import jax
import jax.numpy as jnp
from jax import lax
from jax.sharding import Mesh, PartitionSpec as P

HALF_HEADS = 40
HEAD_DIM = 64
STATE = 128
SPAN = 256
CONV = 4
INNER = 2560
COLS = 2816


def mixing_output(x_heads, b_span, c_span, cumulative, step_size):
    scores = jnp.dot(c_span, b_span.T, preferred_element_type=jnp.float32)
    span_len = cumulative.shape[1]
    causal = jnp.arange(span_len)[:, None] >= jnp.arange(span_len)[None, :]
    spread = jnp.where(causal[None], cumulative[:, :, None] - cumulative[:, None, :], -jnp.inf)
    mixing = (scores[None] * jnp.exp(spread) * step_size[:, None, :]).astype(jnp.bfloat16)
    return jnp.einsum("hqk,khp->qhp", mixing, x_heads, preferred_element_type=jnp.float32)


def span_state(x_heads, b_span, cumulative, step_size):
    weight = jnp.exp(cumulative[:, -1:] - cumulative) * step_size
    decayed = (x_heads * weight.T[:, :, None]).astype(jnp.bfloat16)
    return jnp.einsum("khp,kn->hpn", decayed, b_span, preferred_element_type=jnp.float32)


def state_output(c_span, entering, cumulative):
    readout = jnp.einsum(
        "qn,hpn->qhp", c_span.astype(jnp.float32), entering, precision=lax.Precision.HIGHEST
    )
    return jnp.exp(cumulative).T[:, :, None] * readout


SEQ = ("y", "core")


def shifted(array, by):
    peers = lax.axis_size(SEQ)
    pairs = [(i, i + by) for i in range(peers) if i + by < peers]
    return lax.ppermute(array, SEQ, pairs)


def scan_entering(total, state):
    acc_total, acc_state = shifted(total, 1), shifted(state, 1)
    by = 1
    while by < lax.axis_size(SEQ):
        got_total, got_state = shifted(acc_total, by), shifted(acc_state, by)
        acc_state = jnp.exp(acc_total)[:, None, None] * got_state + acc_state
        acc_total = acc_total + got_total
        by *= 2
    return acc_state


def project(token_rows, input_weight):
    rows = input_weight.shape[0]
    mine = lax.all_gather(input_weight, ("dp", "y"), axis=0, tiled=True)
    other = lax.ppermute(mine, "core", [(0, 1), (1, 0)])
    dims = (((1,), (1,)), ((), ()))
    p_mine = lax.dot_general(token_rows, mine, dims, preferred_element_type=jnp.float32).astype(jnp.bfloat16)
    p_other = lax.dot_general(token_rows, other, dims, preferred_element_type=jnp.float32).astype(jnp.bfloat16)
    first = lax.axis_index("core") == 0
    p0 = jnp.where(first, p_mine, p_other)
    p1 = jnp.where(first, p_other, p_mine)
    length = token_rows.shape[0]
    groups = mine.shape[0] // rows
    return jnp.stack(
        [p0.reshape(length, groups, rows), p1.reshape(length, groups, rows)], axis=2
    ).reshape(length, COLS)


def body(hidden, log_decay, input_weight, conv_weight, conv_bias, skip_gain):
    token_rows = hidden[0]
    length = token_rows.shape[0]
    projected = project(token_rows, input_weight)
    last_rows = projected[length - (CONV - 1) :]
    before_rows = shifted(last_rows, 1)
    extended = jnp.concatenate([before_rows, projected], axis=0)
    filtered = jnp.broadcast_to(conv_bias[None, :], (length, COLS))
    for kernel_tap in range(CONV):
        filtered = (
            filtered
            + extended[kernel_tap : kernel_tap + length].astype(jnp.float32)
            * conv_weight[kernel_tap].astype(jnp.float32)[None, :]
        )
    active = jax.nn.silu(filtered).astype(jnp.bfloat16)
    span_count = length // SPAN
    x_all = active[:, :INNER].reshape(span_count, SPAN, HALF_HEADS, HEAD_DIM)
    b_all = active[:, INNER : INNER + STATE].reshape(span_count, SPAN, STATE)
    c_all = active[:, INNER + STATE :].reshape(span_count, SPAN, STATE)
    decay_spans = log_decay[0].reshape(HALF_HEADS, span_count, SPAN).transpose(1, 0, 2)
    cumulative = jnp.cumsum(decay_spans, axis=2)
    steps_all = -decay_spans
    totals = cumulative[:, :, -1]
    device_total = jnp.sum(totals, axis=0)
    zero_state = jnp.zeros((HALF_HEADS, HEAD_DIM, STATE), jnp.float32)

    def state_of(inputs):
        x_heads, b_span, cum_span, step_span = inputs
        return span_state(x_heads, b_span, cum_span, step_span)

    states = lax.map(state_of, (x_all, b_all, cumulative, steps_all))

    def gather_local(held_state, inputs):
        span_total, state_piece = inputs
        return (jnp.exp(span_total)[:, None, None] * held_state + state_piece, None)

    local_end, _ = lax.scan(gather_local, zero_state, (totals, states))
    entering_dev = scan_entering(device_total, local_end)

    def emit(held_state, inputs):
        x_heads, b_span, c_span, cum_span, step_span, span_total, state_piece = inputs
        outputs = mixing_output(x_heads, b_span, c_span, cum_span, step_span) + state_output(
            c_span, held_state, cum_span
        )
        return (jnp.exp(span_total)[:, None, None] * held_state + state_piece, outputs)

    _, outputs = lax.scan(
        emit, entering_dev, (x_all, b_all, c_all, cumulative, steps_all, totals, states)
    )
    outputs = outputs.reshape(length, HALF_HEADS, HEAD_DIM)
    final = outputs + skip_gain[None, :, None] * x_all.reshape(length, HALF_HEADS, HEAD_DIM).astype(
        jnp.float32
    )
    return final.reshape(1, length, INNER).astype(jnp.bfloat16)


def solution(mesh):
    split = Mesh(mesh.devices.reshape(mesh.shape["dp"], mesh.shape["seq"] // 2, 2), ("dp", "y", "core"))
    placed = (P("dp", SEQ, None), P("dp", None, SEQ), P(("dp",) + SEQ, None), P(), P(), P())
    return jax.shard_map(
        body, mesh=split, in_specs=placed, out_specs=P("dp", SEQ, None), check_vma=False
    )
```

```python
import jax
import jax.numpy as jnp
from jax import lax
from jax.experimental import pallas as pl
from jax.sharding import Mesh, PartitionSpec as P

HALF_HEADS = 40
HEAD_DIM = 64
STATE = 128
SPAN = 256
CONV = 4
INNER = 2560
COLS = 2816
GROUP = 8
SEQ = ("y", "core")


def shifted(array, by):
    peers = lax.axis_size(SEQ)
    pairs = [(i, i + by) for i in range(peers) if i + by < peers]
    return lax.ppermute(array, SEQ, pairs)


def scan_entering(total, state):
    acc_total, acc_state = shifted(total, 1), shifted(state, 1)
    by = 1
    while by < lax.axis_size(SEQ):
        got_total, got_state = shifted(acc_total, by), shifted(acc_state, by)
        acc_state = jnp.exp(acc_total)[:, None, None] * got_state + acc_state
        acc_total = acc_total + got_total
        by *= 2
    return acc_state


def pair_lanes(columns, pair):
    lane = lax.broadcasted_iota(jnp.int32, (columns.shape[0], 2 * HEAD_DIM), 1)
    return jnp.where(lane < HEAD_DIM, columns[:, 2 * pair : 2 * pair + 1], columns[:, 2 * pair + 1 : 2 * pair + 2])


def states_kernel(x_ref, b_ref, cum_ref, step_ref, out_ref):
    cum = cum_ref[0]
    weight = jnp.exp(cum[SPAN - 1 : SPAN, :] - cum) * step_ref[0]
    b_span = b_ref[...]
    for pair in range(GROUP // 2):
        lanes = slice(2 * HEAD_DIM * pair, 2 * HEAD_DIM * (pair + 1))
        decayed = (x_ref[:, lanes].astype(jnp.float32) * pair_lanes(weight, pair)).astype(jnp.bfloat16)
        out_ref[0, lanes, :] = lax.dot_general(
            decayed, b_span, (((0,), (0,)), ((), ())), preferred_element_type=jnp.float32
        )


def output_kernel(x_ref, b_ref, c_ref, cum_ref, cum_row_ref, step_row_ref, enter_ref, gain_ref, out_ref):
    c_span = c_ref[...]
    scores = lax.dot_general(c_span, b_ref[...], (((1,), (1,)), ((), ())), preferred_element_type=jnp.float32)
    causal = lax.broadcasted_iota(jnp.int32, (SPAN, SPAN), 0) >= lax.broadcasted_iota(jnp.int32, (SPAN, SPAN), 1)
    cum = cum_ref[0]
    rise = jnp.exp(cum)
    c32 = c_span.astype(jnp.float32)
    lane = lax.broadcasted_iota(jnp.int32, (SPAN, 2 * HEAD_DIM), 1)
    for pair in range(GROUP // 2):
        lanes = slice(2 * HEAD_DIM * pair, 2 * HEAD_DIM * (pair + 1))
        x_pair = x_ref[:, lanes]
        parts = []
        for half in range(2):
            head = 2 * pair + half
            spread = cum[:, head : head + 1] - cum_row_ref[head : head + 1, :]
            decay = jnp.where(causal, jnp.exp(jnp.where(causal, spread, 0.0)), 0.0)
            mixing = (scores * decay * step_row_ref[head : head + 1, :]).astype(jnp.bfloat16)
            parts.append(jnp.dot(mixing, x_pair, preferred_element_type=jnp.float32))
        intra = jnp.where(lane < HEAD_DIM, parts[0], parts[1])
        readout = lax.dot_general(
            c32, enter_ref[0, lanes, :], (((1,), (1,)), ((), ())),
            precision=lax.Precision.HIGHEST, preferred_element_type=jnp.float32,
        )
        total = intra + pair_lanes(rise, pair) * readout + gain_ref[:, lanes] * x_pair.astype(jnp.float32)
        out_ref[:, lanes] = total.astype(jnp.bfloat16)


def project(token_rows, input_weight):
    rows = input_weight.shape[0]
    mine = lax.all_gather(input_weight, ("dp", "y"), axis=0, tiled=True)
    other = lax.ppermute(mine, "core", [(0, 1), (1, 0)])
    dims = (((1,), (1,)), ((), ()))
    p_mine = lax.dot_general(token_rows, mine, dims, preferred_element_type=jnp.float32).astype(jnp.bfloat16)
    p_other = lax.dot_general(token_rows, other, dims, preferred_element_type=jnp.float32).astype(jnp.bfloat16)
    first = lax.axis_index("core") == 0
    p0 = jnp.where(first, p_mine, p_other)
    p1 = jnp.where(first, p_other, p_mine)
    length = token_rows.shape[0]
    groups = mine.shape[0] // rows
    return jnp.stack(
        [p0.reshape(length, groups, rows), p1.reshape(length, groups, rows)], axis=2
    ).reshape(length, COLS)


def body(hidden, log_decay, input_weight, conv_weight, conv_bias, skip_gain):
    token_rows = hidden[0]
    length = token_rows.shape[0]
    span_count = length // SPAN
    groups = HALF_HEADS // GROUP
    projected = project(token_rows, input_weight)
    before_rows = shifted(projected[length - (CONV - 1) :], 1)
    extended = jnp.concatenate([before_rows, projected], axis=0)
    filtered = jnp.broadcast_to(conv_bias[None, :], (length, COLS))
    for kernel_tap in range(CONV):
        filtered = (
            filtered
            + extended[kernel_tap : kernel_tap + length].astype(jnp.float32)
            * conv_weight[kernel_tap].astype(jnp.float32)[None, :]
        )
    active = jax.nn.silu(filtered).astype(jnp.bfloat16)

    decay = log_decay[0]
    cum_row = jnp.cumsum(decay.reshape(HALF_HEADS, span_count, SPAN), axis=2).reshape(HALF_HEADS, length)
    step_row = -decay
    cum_grouped = cum_row.reshape(groups, GROUP, length).transpose(0, 2, 1)
    step_grouped = step_row.reshape(groups, GROUP, length).transpose(0, 2, 1)
    totals = cum_row.reshape(HALF_HEADS, span_count, SPAN)[:, :, -1].T

    x_spec = pl.BlockSpec((SPAN, GROUP * HEAD_DIM), lambda c, g: (c, g))
    b_spec = pl.BlockSpec((SPAN, STATE), lambda c, g: (c, INNER // STATE))
    c_spec = pl.BlockSpec((SPAN, STATE), lambda c, g: (c, INNER // STATE + 1))
    col_spec = pl.BlockSpec((1, SPAN, GROUP), lambda c, g: (g, c, 0))
    row_spec = pl.BlockSpec((GROUP, SPAN), lambda c, g: (g, c))
    state_spec = pl.BlockSpec((1, GROUP * HEAD_DIM, STATE), lambda c, g: (c, g, 0))
    states = pl.pallas_call(
        states_kernel,
        grid=(span_count, groups),
        in_specs=[x_spec, b_spec, col_spec, col_spec],
        out_specs=state_spec,
        out_shape=jax.ShapeDtypeStruct((span_count, INNER, STATE), jnp.float32),
    )(active, active, cum_grouped, step_grouped)
    states = states.reshape(span_count, HALF_HEADS, HEAD_DIM, STATE)

    local = jnp.zeros((HALF_HEADS, HEAD_DIM, STATE), jnp.float32)
    for span in range(span_count):
        local = jnp.exp(totals[span])[:, None, None] * local + states[span]
    held = scan_entering(jnp.sum(totals, axis=0), local)
    entering = []
    for span in range(span_count):
        entering.append(held)
        held = jnp.exp(totals[span])[:, None, None] * held + states[span]
    entering = jnp.stack(entering).reshape(span_count, INNER, STATE)

    gain = jnp.repeat(skip_gain, HEAD_DIM)[None, :]
    out = pl.pallas_call(
        output_kernel,
        grid=(span_count, groups),
        in_specs=[
            x_spec, b_spec, c_spec, col_spec, row_spec, row_spec, state_spec,
            pl.BlockSpec((1, GROUP * HEAD_DIM), lambda c, g: (0, g)),
        ],
        out_specs=x_spec,
        out_shape=jax.ShapeDtypeStruct((length, INNER), jnp.bfloat16),
    )(active, active, active, cum_grouped, cum_row, step_row, entering, gain)
    return out[None]


def solution(mesh):
    split = Mesh(mesh.devices.reshape(mesh.shape["dp"], mesh.shape["seq"] // 2, 2), ("dp", "y", "core"))
    placed = (P("dp", SEQ, None), P("dp", None, SEQ), P(("dp",) + SEQ, None), P(), P(), P())
    return jax.shard_map(
        body, mesh=split, in_specs=placed, out_specs=P("dp", SEQ, None), check_vma=False
    )
```

```python
import jax
import jax.numpy as jnp
from jax import lax
from jax.experimental import pallas as pl
from jax.sharding import Mesh, PartitionSpec as P

HALF_HEADS = 40
HEAD_DIM = 64
STATE = 128
SPAN = 256
CONV = 4
INNER = 2560
COLS = 2816
GROUP = 8
SEQ = ("y", "core")


def shifted(array, by):
    peers = lax.axis_size(SEQ)
    pairs = [(i, i + by) for i in range(peers) if i + by < peers]
    return lax.ppermute(array, SEQ, pairs)


def swapped(array):
    return lax.ppermute(array, "core", [(0, 1), (1, 0)])


def scan_entering(total, state):
    core = lax.axis_index("core")
    half = HALF_HEADS // 2
    halves = state.reshape(2, half, HEAD_DIM, STATE)
    mine = lax.dynamic_index_in_dim(halves, core, 0, False)
    sent = swapped(lax.dynamic_index_in_dim(halves, 1 - core, 0, False))
    totals = total.reshape(2, half)
    my_total = lax.dynamic_index_in_dim(totals, core, 0, False)
    peer_total = swapped(lax.dynamic_index_in_dim(totals, 1 - core, 0, False))
    first = core == 0
    early_state = jnp.where(first, mine, sent)
    late_state = jnp.where(first, sent, mine)
    early_total = jnp.where(first, my_total, peer_total)
    late_total = jnp.where(first, peer_total, my_total)
    chip_state = jnp.exp(late_total)[:, None, None] * early_state + late_state
    chip_total = early_total + late_total
    chips = lax.axis_size("y")
    held = jnp.zeros_like(chip_state)
    gap = jnp.zeros_like(chip_total)
    for by in range(1, chips):
        pairs = [(i, i + by) for i in range(chips) if i + by < chips]
        got_state = lax.ppermute(chip_state, "y", pairs)
        got_total = lax.ppermute(chip_total, "y", pairs)
        held = held + jnp.exp(gap)[:, None, None] * got_state
        gap = gap + got_total
    later = jnp.exp(early_total)[:, None, None] * held + early_state
    mine_in = jnp.where(first, held, later)
    other_in = swapped(jnp.where(first, later, held))
    return jnp.where(first, jnp.concatenate([mine_in, other_in]), jnp.concatenate([other_in, mine_in]))


def pair_lanes(columns, pair):
    lane = lax.broadcasted_iota(jnp.int32, (columns.shape[0], 2 * HEAD_DIM), 1)
    return jnp.where(lane < HEAD_DIM, columns[:, 2 * pair : 2 * pair + 1], columns[:, 2 * pair + 1 : 2 * pair + 2])


def states_kernel(x_ref, b_ref, cum_ref, step_ref, out_ref):
    cum = cum_ref[0]
    weight = jnp.exp(cum[SPAN - 1 : SPAN, :] - cum) * step_ref[0]
    b_span = b_ref[...]
    for pair in range(GROUP // 2):
        lanes = slice(2 * HEAD_DIM * pair, 2 * HEAD_DIM * (pair + 1))
        decayed = (x_ref[:, lanes].astype(jnp.float32) * pair_lanes(weight, pair)).astype(jnp.bfloat16)
        out_ref[0, lanes, :] = lax.dot_general(
            decayed, b_span, (((0,), (0,)), ((), ())), preferred_element_type=jnp.float32
        )


def output_kernel(x_ref, b_ref, c_ref, cum_ref, cum_row_ref, step_row_ref, enter_ref, gain_ref, out_ref):
    c_span = c_ref[...]
    scores = lax.dot_general(c_span, b_ref[...], (((1,), (1,)), ((), ())), preferred_element_type=jnp.float32)
    causal = lax.broadcasted_iota(jnp.int32, (SPAN, SPAN), 0) >= lax.broadcasted_iota(jnp.int32, (SPAN, SPAN), 1)
    cum = cum_ref[0]
    rise = jnp.exp(cum)
    c32 = c_span.astype(jnp.float32)
    lane = lax.broadcasted_iota(jnp.int32, (SPAN, 2 * HEAD_DIM), 1)
    for pair in range(GROUP // 2):
        lanes = slice(2 * HEAD_DIM * pair, 2 * HEAD_DIM * (pair + 1))
        x_pair = x_ref[:, lanes]
        parts = []
        for half in range(2):
            head = 2 * pair + half
            spread = cum[:, head : head + 1] - cum_row_ref[head : head + 1, :]
            decay = jnp.where(causal, jnp.exp(jnp.where(causal, spread, 0.0)), 0.0)
            mixing = (scores * decay * step_row_ref[head : head + 1, :]).astype(jnp.bfloat16)
            parts.append(jnp.dot(mixing, x_pair, preferred_element_type=jnp.float32))
        intra = jnp.where(lane < HEAD_DIM, parts[0], parts[1])
        readout = lax.dot_general(
            c32, enter_ref[0, lanes, :], (((1,), (1,)), ((), ())),
            precision=lax.Precision.HIGHEST, preferred_element_type=jnp.float32,
        )
        total = intra + pair_lanes(rise, pair) * readout + gain_ref[:, lanes] * x_pair.astype(jnp.float32)
        out_ref[:, lanes] = total.astype(jnp.bfloat16)


def project(token_rows, input_weight):
    return lax.dot_general(
        token_rows,
        lax.all_gather(input_weight, ("dp",) + SEQ, axis=0, tiled=True),
        (((1,), (1,)), ((), ())),
        preferred_element_type=jnp.float32,
    ).astype(jnp.bfloat16)


def body(hidden, log_decay, input_weight, conv_weight, conv_bias, skip_gain):
    token_rows = hidden[0]
    length = token_rows.shape[0]
    span_count = length // SPAN
    groups = HALF_HEADS // GROUP
    projected = project(token_rows, input_weight)
    before_rows = shifted(projected[length - (CONV - 1) :], 1)
    extended = jnp.concatenate([before_rows, projected], axis=0)
    filtered = jnp.broadcast_to(conv_bias[None, :], (length, COLS))
    for kernel_tap in range(CONV):
        filtered = (
            filtered
            + extended[kernel_tap : kernel_tap + length].astype(jnp.float32)
            * conv_weight[kernel_tap].astype(jnp.float32)[None, :]
        )
    active = jax.nn.silu(filtered).astype(jnp.bfloat16)

    decay = log_decay[0]
    cum_row = jnp.cumsum(decay.reshape(HALF_HEADS, span_count, SPAN), axis=2).reshape(HALF_HEADS, length)
    step_row = -decay
    cum_grouped = cum_row.reshape(groups, GROUP, length).transpose(0, 2, 1)
    step_grouped = step_row.reshape(groups, GROUP, length).transpose(0, 2, 1)
    totals = cum_row.reshape(HALF_HEADS, span_count, SPAN)[:, :, -1].T

    x_spec = pl.BlockSpec((SPAN, GROUP * HEAD_DIM), lambda c, g: (c, g))
    b_spec = pl.BlockSpec((SPAN, STATE), lambda c, g: (c, INNER // STATE))
    c_spec = pl.BlockSpec((SPAN, STATE), lambda c, g: (c, INNER // STATE + 1))
    col_spec = pl.BlockSpec((1, SPAN, GROUP), lambda c, g: (g, c, 0))
    row_spec = pl.BlockSpec((GROUP, SPAN), lambda c, g: (g, c))
    state_spec = pl.BlockSpec((1, GROUP * HEAD_DIM, STATE), lambda c, g: (c, g, 0))
    states = pl.pallas_call(
        states_kernel,
        grid=(span_count, groups),
        in_specs=[x_spec, b_spec, col_spec, col_spec],
        out_specs=state_spec,
        out_shape=jax.ShapeDtypeStruct((span_count, INNER, STATE), jnp.float32),
    )(active, active, cum_grouped, step_grouped)
    states = states.reshape(span_count, HALF_HEADS, HEAD_DIM, STATE)

    local = jnp.zeros((HALF_HEADS, HEAD_DIM, STATE), jnp.float32)
    for span in range(span_count):
        local = jnp.exp(totals[span])[:, None, None] * local + states[span]
    held = scan_entering(jnp.sum(totals, axis=0), local)
    entering = []
    for span in range(span_count):
        entering.append(held)
        held = jnp.exp(totals[span])[:, None, None] * held + states[span]
    entering = jnp.stack(entering).reshape(span_count, INNER, STATE)

    gain = jnp.repeat(skip_gain, HEAD_DIM)[None, :]
    out = pl.pallas_call(
        output_kernel,
        grid=(span_count, groups),
        in_specs=[
            x_spec, b_spec, c_spec, col_spec, row_spec, row_spec, state_spec,
            pl.BlockSpec((1, GROUP * HEAD_DIM), lambda c, g: (0, g)),
        ],
        out_specs=x_spec,
        out_shape=jax.ShapeDtypeStruct((length, INNER), jnp.bfloat16),
    )(active, active, active, cum_grouped, cum_row, step_row, entering, gain)
    return out[None]


def solution(mesh):
    split = Mesh(mesh.devices.reshape(mesh.shape["dp"], mesh.shape["seq"] // 2, 2), ("dp", "y", "core"))
    placed = (P("dp", SEQ, None), P("dp", None, SEQ), P(("dp",) + SEQ, None), P(), P(), P())
    return jax.shard_map(
        body, mesh=split, in_specs=placed, out_specs=P("dp", SEQ, None), check_vma=False
    )
```

```python
import jax
import jax.numpy as jnp
from jax import lax
from jax.experimental import pallas as pl
from jax.sharding import Mesh, PartitionSpec as P

HALF_HEADS = 40
HEAD_DIM = 64
STATE = 128
SPAN = 256
CONV = 4
INNER = 2560
COLS = 2816
GROUP = 8
SEQ = ("y", "core")


def shifted(array, by):
    peers = lax.axis_size(SEQ)
    pairs = [(i, i + by) for i in range(peers) if i + by < peers]
    return lax.ppermute(array, SEQ, pairs)


def swapped(array):
    return lax.ppermute(array, "core", [(0, 1), (1, 0)])


def scan_entering(total, state, side, side_inputs):
    core = lax.axis_index("core")
    half = HALF_HEADS // 2
    halves = state.reshape(2, half, HEAD_DIM, STATE)
    mine = lax.dynamic_index_in_dim(halves, core, 0, False)
    sent = swapped(lax.dynamic_index_in_dim(halves, 1 - core, 0, False))
    totals = total.reshape(2, half)
    my_total = lax.dynamic_index_in_dim(totals, core, 0, False)
    peer_total = swapped(lax.dynamic_index_in_dim(totals, 1 - core, 0, False))
    first = core == 0
    early_state = jnp.where(first, mine, sent)
    late_state = jnp.where(first, sent, mine)
    early_total = jnp.where(first, my_total, peer_total)
    late_total = jnp.where(first, peer_total, my_total)
    chip_state = jnp.exp(late_total)[:, None, None] * early_state + late_state
    chip_total = early_total + late_total
    chips = lax.axis_size("y")
    chip_state, chip_total, side_inputs = lax.optimization_barrier((chip_state, chip_total, side_inputs))
    got = []
    for by in range(1, chips):
        pairs = [(i, i + by) for i in range(chips) if i + by < chips]
        got.append((lax.ppermute(chip_state, "y", pairs), lax.ppermute(chip_total, "y", pairs)))
    side_out = side(*side_inputs)
    got, side_out = lax.optimization_barrier((got, side_out))
    held = jnp.zeros_like(chip_state)
    gap = jnp.zeros_like(chip_total)
    for got_state, got_total in got:
        held = held + jnp.exp(gap)[:, None, None] * got_state
        gap = gap + got_total
    later = jnp.exp(early_total)[:, None, None] * held + early_state
    mine_in = jnp.where(first, held, later)
    other_in = swapped(jnp.where(first, later, held))
    return jnp.where(first, jnp.concatenate([mine_in, other_in]), jnp.concatenate([other_in, mine_in])), side_out


def pair_lanes(columns, pair):
    lane = lax.broadcasted_iota(jnp.int32, (columns.shape[0], 2 * HEAD_DIM), 1)
    return jnp.where(lane < HEAD_DIM, columns[:, 2 * pair : 2 * pair + 1], columns[:, 2 * pair + 1 : 2 * pair + 2])


def states_kernel(x_ref, b_ref, cum_ref, step_ref, out_ref):
    cum = cum_ref[0]
    weight = jnp.exp(cum[SPAN - 1 : SPAN, :] - cum) * step_ref[0]
    b_span = b_ref[...]
    for pair in range(GROUP // 2):
        lanes = slice(2 * HEAD_DIM * pair, 2 * HEAD_DIM * (pair + 1))
        decayed = (x_ref[:, lanes].astype(jnp.float32) * pair_lanes(weight, pair)).astype(jnp.bfloat16)
        out_ref[0, lanes, :] = lax.dot_general(
            decayed, b_span, (((0,), (0,)), ((), ())), preferred_element_type=jnp.float32
        )


def intra_kernel(x_ref, b_ref, c_ref, cum_ref, cum_row_ref, step_row_ref, gain_ref, part_ref):
    scores = lax.dot_general(c_ref[...], b_ref[...], (((1,), (1,)), ((), ())), preferred_element_type=jnp.float32)
    causal = lax.broadcasted_iota(jnp.int32, (SPAN, SPAN), 0) >= lax.broadcasted_iota(jnp.int32, (SPAN, SPAN), 1)
    cum = cum_ref[0]
    lane = lax.broadcasted_iota(jnp.int32, (SPAN, 2 * HEAD_DIM), 1)
    for pair in range(GROUP // 2):
        lanes = slice(2 * HEAD_DIM * pair, 2 * HEAD_DIM * (pair + 1))
        x_pair = x_ref[:, lanes]
        parts = []
        for half in range(2):
            head = 2 * pair + half
            spread = cum[:, head : head + 1] - cum_row_ref[head : head + 1, :]
            decay = jnp.where(causal, jnp.exp(jnp.where(causal, spread, 0.0)), 0.0)
            mixing = (scores * decay * step_row_ref[head : head + 1, :]).astype(jnp.bfloat16)
            parts.append(jnp.dot(mixing, x_pair, preferred_element_type=jnp.float32))
        intra = jnp.where(lane < HEAD_DIM, parts[0], parts[1])
        part_ref[:, lanes] = intra + gain_ref[:, lanes] * x_pair.astype(jnp.float32)


def readout_kernel(part_ref, c_ref, cum_ref, enter_ref, out_ref):
    rise = jnp.exp(cum_ref[0])
    c32 = c_ref[...].astype(jnp.float32)
    for pair in range(GROUP // 2):
        lanes = slice(2 * HEAD_DIM * pair, 2 * HEAD_DIM * (pair + 1))
        readout = lax.dot_general(
            c32, enter_ref[0, lanes, :], (((1,), (1,)), ((), ())),
            precision=lax.Precision.HIGHEST, preferred_element_type=jnp.float32,
        )
        out_ref[:, lanes] = (part_ref[:, lanes] + pair_lanes(rise, pair) * readout).astype(jnp.bfloat16)


def project(token_rows, input_weight, chunks=4):
    width = token_rows.shape[1] // chunks
    total = None
    for chunk in range(chunks):
        cols = slice(chunk * width, (chunk + 1) * width)
        weight = lax.all_gather(input_weight[:, cols], ("dp",) + SEQ, axis=0, tiled=True)
        piece = lax.dot_general(
            token_rows[:, cols], weight, (((1,), (1,)), ((), ())), preferred_element_type=jnp.float32
        )
        total = piece if total is None else total + piece
    return total.astype(jnp.bfloat16)


def body(hidden, log_decay, input_weight, conv_weight, conv_bias, skip_gain):
    token_rows = hidden[0]
    length = token_rows.shape[0]
    span_count = length // SPAN
    groups = HALF_HEADS // GROUP
    projected = project(token_rows, input_weight)
    before_rows = shifted(projected[length - (CONV - 1) :], 1)
    extended = jnp.concatenate([before_rows, projected], axis=0)
    filtered = jnp.broadcast_to(conv_bias[None, :], (length, COLS))
    for kernel_tap in range(CONV):
        filtered = (
            filtered
            + extended[kernel_tap : kernel_tap + length].astype(jnp.float32)
            * conv_weight[kernel_tap].astype(jnp.float32)[None, :]
        )
    active = jax.nn.silu(filtered).astype(jnp.bfloat16)

    decay = log_decay[0]
    cum_row = jnp.cumsum(decay.reshape(HALF_HEADS, span_count, SPAN), axis=2).reshape(HALF_HEADS, length)
    step_row = -decay
    cum_grouped = cum_row.reshape(groups, GROUP, length).transpose(0, 2, 1)
    step_grouped = step_row.reshape(groups, GROUP, length).transpose(0, 2, 1)
    totals = cum_row.reshape(HALF_HEADS, span_count, SPAN)[:, :, -1].T

    x_spec = pl.BlockSpec((SPAN, GROUP * HEAD_DIM), lambda c, g: (c, g))
    b_spec = pl.BlockSpec((SPAN, STATE), lambda c, g: (c, INNER // STATE))
    c_spec = pl.BlockSpec((SPAN, STATE), lambda c, g: (c, INNER // STATE + 1))
    col_spec = pl.BlockSpec((1, SPAN, GROUP), lambda c, g: (g, c, 0))
    row_spec = pl.BlockSpec((GROUP, SPAN), lambda c, g: (g, c))
    state_spec = pl.BlockSpec((1, GROUP * HEAD_DIM, STATE), lambda c, g: (c, g, 0))
    gain = jnp.repeat(skip_gain, HEAD_DIM)[None, :]
    gain_spec = pl.BlockSpec((1, GROUP * HEAD_DIM), lambda c, g: (0, g))
    states = pl.pallas_call(
        states_kernel,
        grid=(span_count, groups),
        in_specs=[x_spec, b_spec, col_spec, col_spec],
        out_specs=state_spec,
        out_shape=jax.ShapeDtypeStruct((span_count, INNER, STATE), jnp.float32),
        cost_estimate=pl.CostEstimate(
            flops=2 * length * INNER * STATE, transcendentals=length * HALF_HEADS,
            bytes_accessed=2 * length * (INNER + STATE) + 4 * span_count * INNER * STATE,
        ),
    )(active, active, cum_grouped, step_grouped)
    states = states.reshape(span_count, HALF_HEADS, HEAD_DIM, STATE)

    local = jnp.zeros((HALF_HEADS, HEAD_DIM, STATE), jnp.float32)
    for span in range(span_count):
        local = jnp.exp(totals[span])[:, None, None] * local + states[span]
    def intra(active, cum_grouped, cum_row, step_row, gain):
        return pl.pallas_call(
            intra_kernel,
            grid=(span_count, groups),
            in_specs=[x_spec, b_spec, c_spec, col_spec, row_spec, row_spec, gain_spec],
            out_specs=x_spec,
            out_shape=jax.ShapeDtypeStruct((length, INNER), jnp.float32),
            cost_estimate=pl.CostEstimate(
                flops=2 * length * SPAN * (groups * STATE + 2 * INNER), transcendentals=length * SPAN * HALF_HEADS,
                bytes_accessed=2 * length * (INNER + 2 * STATE) + 4 * length * INNER,
            ),
        )(active, active, active, cum_grouped, cum_row, step_row, gain)

    held, part = scan_entering(
        jnp.sum(totals, axis=0), local, intra, (active, cum_grouped, cum_row, step_row, gain)
    )
    entering = []
    for span in range(span_count):
        entering.append(held)
        held = jnp.exp(totals[span])[:, None, None] * held + states[span]
    entering = jnp.stack(entering).reshape(span_count, INNER, STATE)

    out = pl.pallas_call(
        readout_kernel,
        grid=(span_count, groups),
        in_specs=[x_spec, c_spec, col_spec, state_spec],
        out_specs=x_spec,
        out_shape=jax.ShapeDtypeStruct((length, INNER), jnp.bfloat16),
        cost_estimate=pl.CostEstimate(
            flops=12 * length * STATE * INNER, transcendentals=length * HALF_HEADS,
            bytes_accessed=6 * length * INNER + 4 * span_count * INNER * STATE,
        ),
    )(part, active, cum_grouped, entering)
    return out[None]


def solution(mesh):
    split = Mesh(mesh.devices.reshape(mesh.shape["dp"], mesh.shape["seq"] // 2, 2), ("dp", "y", "core"))
    placed = (P("dp", SEQ, None), P("dp", None, SEQ), P(("dp",) + SEQ, None), P(), P(), P())
    return jax.shard_map(
        body, mesh=split, in_specs=placed, out_specs=P("dp", SEQ, None), check_vma=False
    )
```

```python
import jax
import jax.numpy as jnp
from jax import lax
from jax.experimental import pallas as pl
from jax.sharding import Mesh, PartitionSpec as P

HALF_HEADS = 40
HEAD_DIM = 64
STATE = 128
SPAN = 256
CONV = 4
INNER = 2560
COLS = 2816
GROUP = 8
SEQ = ("y", "core")
DP = ("z", "x")


def shifted(array, by):
    peers = lax.axis_size(SEQ)
    pairs = [(i, i + by) for i in range(peers) if i + by < peers]
    return lax.ppermute(array, SEQ, pairs)


def swapped(array):
    return lax.ppermute(array, "core", [(0, 1), (1, 0)])


def scan_entering(total, state, side, side_inputs):
    core = lax.axis_index("core")
    half = HALF_HEADS // 2
    halves = state.reshape(2, half, HEAD_DIM, STATE)
    mine = lax.dynamic_index_in_dim(halves, core, 0, False)
    sent = swapped(lax.dynamic_index_in_dim(halves, 1 - core, 0, False))
    totals = total.reshape(2, half)
    my_total = lax.dynamic_index_in_dim(totals, core, 0, False)
    peer_total = swapped(lax.dynamic_index_in_dim(totals, 1 - core, 0, False))
    first = core == 0
    early_state = jnp.where(first, mine, sent)
    late_state = jnp.where(first, sent, mine)
    early_total = jnp.where(first, my_total, peer_total)
    late_total = jnp.where(first, peer_total, my_total)
    chip_state = jnp.exp(late_total)[:, None, None] * early_state + late_state
    chip_total = early_total + late_total
    chips = lax.axis_size("y")
    chip_state, chip_total, side_inputs = lax.optimization_barrier((chip_state, chip_total, side_inputs))
    got = []
    for by in range(1, chips):
        pairs = [(i, i + by) for i in range(chips) if i + by < chips]
        got.append((lax.ppermute(chip_state, "y", pairs), lax.ppermute(chip_total, "y", pairs)))
    side_out = side(*side_inputs)
    got, side_out = lax.optimization_barrier((got, side_out))
    held = jnp.zeros_like(chip_state)
    gap = jnp.zeros_like(chip_total)
    for got_state, got_total in got:
        held = held + jnp.exp(gap)[:, None, None] * got_state
        gap = gap + got_total
    later = jnp.exp(early_total)[:, None, None] * held + early_state
    mine_in = jnp.where(first, held, later)
    other_in = swapped(jnp.where(first, later, held))
    return jnp.where(first, jnp.concatenate([mine_in, other_in]), jnp.concatenate([other_in, mine_in])), side_out


def pair_lanes(columns, pair):
    lane = lax.broadcasted_iota(jnp.int32, (columns.shape[0], 2 * HEAD_DIM), 1)
    return jnp.where(lane < HEAD_DIM, columns[:, 2 * pair : 2 * pair + 1], columns[:, 2 * pair + 1 : 2 * pair + 2])


def states_kernel(x_ref, b_ref, cum_ref, step_ref, out_ref):
    cum = cum_ref[0]
    weight = jnp.exp(cum[SPAN - 1 : SPAN, :] - cum) * step_ref[0]
    b_span = b_ref[...]
    for pair in range(GROUP // 2):
        lanes = slice(2 * HEAD_DIM * pair, 2 * HEAD_DIM * (pair + 1))
        decayed = (x_ref[:, lanes].astype(jnp.float32) * pair_lanes(weight, pair)).astype(jnp.bfloat16)
        out_ref[0, lanes, :] = lax.dot_general(
            decayed, b_span, (((0,), (0,)), ((), ())), preferred_element_type=jnp.float32
        )


def intra_kernel(x_ref, b_ref, c_ref, cum_ref, cum_row_ref, step_row_ref, gain_ref, part_ref):
    scores = lax.dot_general(c_ref[...], b_ref[...], (((1,), (1,)), ((), ())), preferred_element_type=jnp.float32)
    causal = lax.broadcasted_iota(jnp.int32, (SPAN, SPAN), 0) >= lax.broadcasted_iota(jnp.int32, (SPAN, SPAN), 1)
    cum = cum_ref[0]
    lane = lax.broadcasted_iota(jnp.int32, (SPAN, 2 * HEAD_DIM), 1)
    for pair in range(GROUP // 2):
        lanes = slice(2 * HEAD_DIM * pair, 2 * HEAD_DIM * (pair + 1))
        x_pair = x_ref[:, lanes]
        parts = []
        for half in range(2):
            head = 2 * pair + half
            spread = cum[:, head : head + 1] - cum_row_ref[head : head + 1, :]
            decay = jnp.where(causal, jnp.exp(jnp.where(causal, spread, 0.0)), 0.0)
            mixing = (scores * decay * step_row_ref[head : head + 1, :]).astype(jnp.bfloat16)
            parts.append(jnp.dot(mixing, x_pair, preferred_element_type=jnp.float32))
        intra = jnp.where(lane < HEAD_DIM, parts[0], parts[1])
        part_ref[:, lanes] = intra + gain_ref[:, lanes] * x_pair.astype(jnp.float32)


def readout_kernel(part_ref, c_ref, cum_ref, enter_ref, out_ref):
    rise = jnp.exp(cum_ref[0])
    c32 = c_ref[...].astype(jnp.float32)
    for pair in range(GROUP // 2):
        lanes = slice(2 * HEAD_DIM * pair, 2 * HEAD_DIM * (pair + 1))
        readout = lax.dot_general(
            c32, enter_ref[0, lanes, :], (((1,), (1,)), ((), ())),
            precision=lax.Precision.HIGHEST, preferred_element_type=jnp.float32,
        )
        out_ref[:, lanes] = (part_ref[:, lanes] + pair_lanes(rise, pair) * readout).astype(jnp.bfloat16)


def gathered_along(piece, axis):
    n = lax.axis_size(axis)
    if n == 1:
        return piece
    place = lax.axis_index(axis)
    got = [piece] + [lax.ppermute(piece, axis, [(i, (i + s) % n) for i in range(n)]) for s in range(1, n)]
    ring = jnp.stack(got[::-1])
    rows = lax.dynamic_slice_in_dim(jnp.concatenate([ring, ring]), n - 1 - place, n, axis=0)
    return rows.reshape((n * piece.shape[0],) + piece.shape[1:])


def full_weight(local):
    mine = gathered_along(gathered_along(gathered_along(local, "y"), "x"), "z")
    other = lax.ppermute(mine, "core", [(0, 1), (1, 0)])
    first = lax.axis_index("core") == 0
    pieces = mine.shape[0] // local.shape[0]
    early = jnp.where(first, mine, other).reshape((pieces, 1) + local.shape)
    late = jnp.where(first, other, mine).reshape((pieces, 1) + local.shape)
    return jnp.concatenate([early, late], axis=1).reshape((-1,) + local.shape[1:])


def project(token_rows, input_weight):
    return lax.dot_general(
        token_rows, full_weight(input_weight), (((1,), (1,)), ((), ())), preferred_element_type=jnp.float32
    ).astype(jnp.bfloat16)


def body(hidden, log_decay, input_weight, conv_weight, conv_bias, skip_gain):
    token_rows = hidden[0]
    length = token_rows.shape[0]
    span_count = length // SPAN
    groups = HALF_HEADS // GROUP
    projected = project(token_rows, input_weight)
    before_rows = shifted(projected[length - (CONV - 1) :], 1)
    extended = jnp.concatenate([before_rows, projected], axis=0)
    filtered = jnp.broadcast_to(conv_bias[None, :], (length, COLS))
    for kernel_tap in range(CONV):
        filtered = (
            filtered
            + extended[kernel_tap : kernel_tap + length].astype(jnp.float32)
            * conv_weight[kernel_tap].astype(jnp.float32)[None, :]
        )
    active = jax.nn.silu(filtered).astype(jnp.bfloat16)

    decay = log_decay[0]
    cum_row = jnp.cumsum(decay.reshape(HALF_HEADS, span_count, SPAN), axis=2).reshape(HALF_HEADS, length)
    step_row = -decay
    cum_grouped = cum_row.reshape(groups, GROUP, length).transpose(0, 2, 1)
    step_grouped = step_row.reshape(groups, GROUP, length).transpose(0, 2, 1)
    totals = cum_row.reshape(HALF_HEADS, span_count, SPAN)[:, :, -1].T

    x_spec = pl.BlockSpec((SPAN, GROUP * HEAD_DIM), lambda c, g: (c, g))
    b_spec = pl.BlockSpec((SPAN, STATE), lambda c, g: (c, INNER // STATE))
    c_spec = pl.BlockSpec((SPAN, STATE), lambda c, g: (c, INNER // STATE + 1))
    col_spec = pl.BlockSpec((1, SPAN, GROUP), lambda c, g: (g, c, 0))
    row_spec = pl.BlockSpec((GROUP, SPAN), lambda c, g: (g, c))
    state_spec = pl.BlockSpec((1, GROUP * HEAD_DIM, STATE), lambda c, g: (c, g, 0))
    gain = jnp.repeat(skip_gain, HEAD_DIM)[None, :]
    gain_spec = pl.BlockSpec((1, GROUP * HEAD_DIM), lambda c, g: (0, g))
    states = pl.pallas_call(
        states_kernel,
        grid=(span_count, groups),
        in_specs=[x_spec, b_spec, col_spec, col_spec],
        out_specs=state_spec,
        out_shape=jax.ShapeDtypeStruct((span_count, INNER, STATE), jnp.float32),
        cost_estimate=pl.CostEstimate(
            flops=2 * length * INNER * STATE, transcendentals=length * HALF_HEADS,
            bytes_accessed=2 * length * (INNER + STATE) + 4 * span_count * INNER * STATE,
        ),
    )(active, active, cum_grouped, step_grouped)
    states = states.reshape(span_count, HALF_HEADS, HEAD_DIM, STATE)

    local = jnp.zeros((HALF_HEADS, HEAD_DIM, STATE), jnp.float32)
    for span in range(span_count):
        local = jnp.exp(totals[span])[:, None, None] * local + states[span]
    def intra(active, cum_grouped, cum_row, step_row, gain):
        return pl.pallas_call(
            intra_kernel,
            grid=(span_count, groups),
            in_specs=[x_spec, b_spec, c_spec, col_spec, row_spec, row_spec, gain_spec],
            out_specs=x_spec,
            out_shape=jax.ShapeDtypeStruct((length, INNER), jnp.float32),
            cost_estimate=pl.CostEstimate(
                flops=2 * length * SPAN * (groups * STATE + 2 * INNER), transcendentals=length * SPAN * HALF_HEADS,
                bytes_accessed=2 * length * (INNER + 2 * STATE) + 4 * length * INNER,
            ),
        )(active, active, active, cum_grouped, cum_row, step_row, gain)

    held, part = scan_entering(
        jnp.sum(totals, axis=0), local, intra, (active, cum_grouped, cum_row, step_row, gain)
    )
    entering = []
    for span in range(span_count):
        entering.append(held)
        held = jnp.exp(totals[span])[:, None, None] * held + states[span]
    entering = jnp.stack(entering).reshape(span_count, INNER, STATE)

    out = pl.pallas_call(
        readout_kernel,
        grid=(span_count, groups),
        in_specs=[x_spec, c_spec, col_spec, state_spec],
        out_specs=x_spec,
        out_shape=jax.ShapeDtypeStruct((length, INNER), jnp.bfloat16),
        cost_estimate=pl.CostEstimate(
            flops=12 * length * STATE * INNER, transcendentals=length * HALF_HEADS,
            bytes_accessed=6 * length * INNER + 4 * span_count * INNER * STATE,
        ),
    )(part, active, cum_grouped, entering)
    return out[None]


def solution(mesh):
    contexts = mesh.shape["dp"]
    across = 4 if contexts % 4 == 0 else 1
    split = Mesh(
        mesh.devices.reshape(contexts // across, across, mesh.shape["seq"] // 2, 2), ("z", "x", "y", "core")
    )
    placed = (P(DP, SEQ, None), P(DP, None, SEQ), P(DP + SEQ, None), P(), P(), P())
    return jax.shard_map(
        body, mesh=split, in_specs=placed, out_specs=P(DP, SEQ, None), check_vma=False
    )
```

```python
import jax
import jax.numpy as jnp
from jax import lax
from jax.experimental import pallas as pl
from jax.sharding import Mesh, PartitionSpec as P

HALF_HEADS = 40
HEAD_DIM = 64
STATE = 128
SPAN = 256
CONV = 4
INNER = 2560
COLS = 2816
GROUP = 8
SEQ = ("y", "core")


def shifted(array, by):
    peers = lax.axis_size(SEQ)
    pairs = [(i, i + by) for i in range(peers) if i + by < peers]
    return lax.ppermute(array, SEQ, pairs)


def swapped(array):
    return lax.ppermute(array, "core", [(0, 1), (1, 0)])


def scan_entering(total, state, side, side_inputs):
    core = lax.axis_index("core")
    half = HALF_HEADS // 2
    halves = state.reshape(2, half, HEAD_DIM, STATE)
    mine = lax.dynamic_index_in_dim(halves, core, 0, False)
    sent = swapped(lax.dynamic_index_in_dim(halves, 1 - core, 0, False))
    totals = total.reshape(2, half)
    my_total = lax.dynamic_index_in_dim(totals, core, 0, False)
    peer_total = swapped(lax.dynamic_index_in_dim(totals, 1 - core, 0, False))
    first = core == 0
    early_state = jnp.where(first, mine, sent)
    late_state = jnp.where(first, sent, mine)
    early_total = jnp.where(first, my_total, peer_total)
    late_total = jnp.where(first, peer_total, my_total)
    chip_state = jnp.exp(late_total)[:, None, None] * early_state + late_state
    chip_total = early_total + late_total
    chips = lax.axis_size("y")
    chip_state, chip_total, side_inputs = lax.optimization_barrier((chip_state, chip_total, side_inputs))
    got = []
    for by in range(1, chips):
        pairs = [(i, i + by) for i in range(chips) if i + by < chips]
        got.append((lax.ppermute(chip_state, "y", pairs), lax.ppermute(chip_total, "y", pairs)))
    side_out = side(*side_inputs)
    got, side_out = lax.optimization_barrier((got, side_out))
    held = jnp.zeros_like(chip_state)
    gap = jnp.zeros_like(chip_total)
    for got_state, got_total in got:
        held = held + jnp.exp(gap)[:, None, None] * got_state
        gap = gap + got_total
    later = jnp.exp(early_total)[:, None, None] * held + early_state
    mine_in = jnp.where(first, held, later)
    other_in = swapped(jnp.where(first, later, held))
    return jnp.where(first, jnp.concatenate([mine_in, other_in]), jnp.concatenate([other_in, mine_in])), side_out


def pair_lanes(columns, pair):
    lane = lax.broadcasted_iota(jnp.int32, (columns.shape[0], 2 * HEAD_DIM), 1)
    return jnp.where(lane < HEAD_DIM, columns[:, 2 * pair : 2 * pair + 1], columns[:, 2 * pair + 1 : 2 * pair + 2])


def states_kernel(x_ref, b_ref, cum_ref, step_ref, out_ref):
    cum = cum_ref[0]
    weight = jnp.exp(cum[SPAN - 1 : SPAN, :] - cum) * step_ref[0]
    b_span = b_ref[...]
    for pair in range(GROUP // 2):
        lanes = slice(2 * HEAD_DIM * pair, 2 * HEAD_DIM * (pair + 1))
        decayed = (x_ref[:, lanes].astype(jnp.float32) * pair_lanes(weight, pair)).astype(jnp.bfloat16)
        out_ref[0, lanes, :] = lax.dot_general(
            decayed, b_span, (((0,), (0,)), ((), ())), preferred_element_type=jnp.float32
        )


def intra_kernel(x_ref, b_ref, c_ref, cum_ref, cum_row_ref, step_row_ref, gain_ref, part_ref):
    scores = lax.dot_general(c_ref[...], b_ref[...], (((1,), (1,)), ((), ())), preferred_element_type=jnp.float32)
    causal = lax.broadcasted_iota(jnp.int32, (SPAN, SPAN), 0) >= lax.broadcasted_iota(jnp.int32, (SPAN, SPAN), 1)
    cum = cum_ref[0]
    lane = lax.broadcasted_iota(jnp.int32, (SPAN, 2 * HEAD_DIM), 1)
    for pair in range(GROUP // 2):
        lanes = slice(2 * HEAD_DIM * pair, 2 * HEAD_DIM * (pair + 1))
        x_pair = x_ref[:, lanes]
        parts = []
        for half in range(2):
            head = 2 * pair + half
            spread = cum[:, head : head + 1] - cum_row_ref[head : head + 1, :]
            decay = jnp.where(causal, jnp.exp(jnp.where(causal, spread, 0.0)), 0.0)
            mixing = (scores * decay * step_row_ref[head : head + 1, :]).astype(jnp.bfloat16)
            parts.append(jnp.dot(mixing, x_pair, preferred_element_type=jnp.float32))
        intra = jnp.where(lane < HEAD_DIM, parts[0], parts[1])
        part_ref[:, lanes] = intra + gain_ref[:, lanes] * x_pair.astype(jnp.float32)


def readout_kernel(part_ref, c_ref, cum_ref, enter_ref, out_ref):
    rise = jnp.exp(cum_ref[0])
    c32 = c_ref[...].astype(jnp.float32)
    for pair in range(GROUP // 2):
        lanes = slice(2 * HEAD_DIM * pair, 2 * HEAD_DIM * (pair + 1))
        readout = lax.dot_general(
            c32, enter_ref[0, lanes, :], (((1,), (1,)), ((), ())),
            precision=lax.Precision.HIGHEST, preferred_element_type=jnp.float32,
        )
        out_ref[:, lanes] = (part_ref[:, lanes] + pair_lanes(rise, pair) * readout).astype(jnp.bfloat16)


def project(token_rows, input_weight):
    weight = lax.all_gather(input_weight, ("dp",) + SEQ, axis=0, tiled=False)
    flipped = lax.dot_general(weight, token_rows, (((2,), (1,)), ((), ())), preferred_element_type=jnp.float32)
    return flipped.astype(jnp.bfloat16).reshape(COLS, token_rows.shape[0]).T


def body(hidden, log_decay, input_weight, conv_weight, conv_bias, skip_gain):
    token_rows = hidden[0]
    length = token_rows.shape[0]
    span_count = length // SPAN
    groups = HALF_HEADS // GROUP
    projected = project(token_rows, input_weight)
    before_rows = shifted(projected[length - (CONV - 1) :], 1)
    extended = jnp.concatenate([before_rows, projected], axis=0)
    filtered = jnp.broadcast_to(conv_bias[None, :], (length, COLS))
    for kernel_tap in range(CONV):
        filtered = (
            filtered
            + extended[kernel_tap : kernel_tap + length].astype(jnp.float32)
            * conv_weight[kernel_tap].astype(jnp.float32)[None, :]
        )
    active = jax.nn.silu(filtered).astype(jnp.bfloat16)

    decay = log_decay[0]
    cum_row = jnp.cumsum(decay.reshape(HALF_HEADS, span_count, SPAN), axis=2).reshape(HALF_HEADS, length)
    step_row = -decay
    cum_grouped = cum_row.reshape(groups, GROUP, length).transpose(0, 2, 1)
    step_grouped = step_row.reshape(groups, GROUP, length).transpose(0, 2, 1)
    totals = cum_row.reshape(HALF_HEADS, span_count, SPAN)[:, :, -1].T

    x_spec = pl.BlockSpec((SPAN, GROUP * HEAD_DIM), lambda c, g: (c, g))
    b_spec = pl.BlockSpec((SPAN, STATE), lambda c, g: (c, INNER // STATE))
    c_spec = pl.BlockSpec((SPAN, STATE), lambda c, g: (c, INNER // STATE + 1))
    col_spec = pl.BlockSpec((1, SPAN, GROUP), lambda c, g: (g, c, 0))
    row_spec = pl.BlockSpec((GROUP, SPAN), lambda c, g: (g, c))
    state_spec = pl.BlockSpec((1, GROUP * HEAD_DIM, STATE), lambda c, g: (c, g, 0))
    gain = jnp.repeat(skip_gain, HEAD_DIM)[None, :]
    gain_spec = pl.BlockSpec((1, GROUP * HEAD_DIM), lambda c, g: (0, g))
    states = pl.pallas_call(
        states_kernel,
        grid=(span_count, groups),
        in_specs=[x_spec, b_spec, col_spec, col_spec],
        out_specs=state_spec,
        out_shape=jax.ShapeDtypeStruct((span_count, INNER, STATE), jnp.float32),
        cost_estimate=pl.CostEstimate(
            flops=2 * length * INNER * STATE, transcendentals=length * HALF_HEADS,
            bytes_accessed=2 * length * (INNER + STATE) + 4 * span_count * INNER * STATE,
        ),
    )(active, active, cum_grouped, step_grouped)
    states = states.reshape(span_count, HALF_HEADS, HEAD_DIM, STATE)

    local = jnp.zeros((HALF_HEADS, HEAD_DIM, STATE), jnp.float32)
    for span in range(span_count):
        local = jnp.exp(totals[span])[:, None, None] * local + states[span]
    def intra(active, cum_grouped, cum_row, step_row, gain):
        return pl.pallas_call(
            intra_kernel,
            grid=(span_count, groups),
            in_specs=[x_spec, b_spec, c_spec, col_spec, row_spec, row_spec, gain_spec],
            out_specs=x_spec,
            out_shape=jax.ShapeDtypeStruct((length, INNER), jnp.float32),
            cost_estimate=pl.CostEstimate(
                flops=2 * length * SPAN * (groups * STATE + 2 * INNER), transcendentals=length * SPAN * HALF_HEADS,
                bytes_accessed=2 * length * (INNER + 2 * STATE) + 4 * length * INNER,
            ),
        )(active, active, active, cum_grouped, cum_row, step_row, gain)

    held, part = scan_entering(
        jnp.sum(totals, axis=0), local, intra, (active, cum_grouped, cum_row, step_row, gain)
    )
    entering = []
    for span in range(span_count):
        entering.append(held)
        held = jnp.exp(totals[span])[:, None, None] * held + states[span]
    entering = jnp.stack(entering).reshape(span_count, INNER, STATE)

    out = pl.pallas_call(
        readout_kernel,
        grid=(span_count, groups),
        in_specs=[x_spec, c_spec, col_spec, state_spec],
        out_specs=x_spec,
        out_shape=jax.ShapeDtypeStruct((length, INNER), jnp.bfloat16),
        cost_estimate=pl.CostEstimate(
            flops=12 * length * STATE * INNER, transcendentals=length * HALF_HEADS,
            bytes_accessed=6 * length * INNER + 4 * span_count * INNER * STATE,
        ),
    )(part, active, cum_grouped, entering)
    return out[None]


def solution(mesh):
    split = Mesh(mesh.devices.reshape(mesh.shape["dp"], mesh.shape["seq"] // 2, 2), ("dp", "y", "core"))
    placed = (P("dp", SEQ, None), P("dp", None, SEQ), P(("dp",) + SEQ, None), P(), P(), P())
    return jax.shard_map(
        body, mesh=split, in_specs=placed, out_specs=P("dp", SEQ, None), check_vma=False
    )
```

```python
import jax
import jax.numpy as jnp
from jax import lax
from jax.experimental import pallas as pl
from jax.sharding import Mesh, PartitionSpec as P

HALF_HEADS = 40
HEAD_DIM = 64
STATE = 128
SPAN = 256
CONV = 4
INNER = 2560
COLS = 2816
GROUP = 8
SEQ = ("y", "core")


def shifted(array, by):
    peers = lax.axis_size(SEQ)
    pairs = [(i, i + by) for i in range(peers) if i + by < peers]
    return lax.ppermute(array, SEQ, pairs)


def swapped(array):
    return lax.ppermute(array, "core", [(0, 1), (1, 0)])


def scan_entering(total, state, side, side_inputs):
    core = lax.axis_index("core")
    half = HALF_HEADS // 2
    halves = state.reshape(2, half, HEAD_DIM, STATE)
    mine = lax.dynamic_index_in_dim(halves, core, 0, False)
    sent = swapped(lax.dynamic_index_in_dim(halves, 1 - core, 0, False))
    totals = total.reshape(2, half)
    my_total = lax.dynamic_index_in_dim(totals, core, 0, False)
    peer_total = swapped(lax.dynamic_index_in_dim(totals, 1 - core, 0, False))
    first = core == 0
    early_state = jnp.where(first, mine, sent)
    late_state = jnp.where(first, sent, mine)
    early_total = jnp.where(first, my_total, peer_total)
    late_total = jnp.where(first, peer_total, my_total)
    chip_state = jnp.exp(late_total)[:, None, None] * early_state + late_state
    chip_total = early_total + late_total
    chips = lax.axis_size("y")
    chip_state, chip_total, side_inputs = lax.optimization_barrier((chip_state, chip_total, side_inputs))
    got = []
    for by in range(1, chips):
        pairs = [(i, i + by) for i in range(chips) if i + by < chips]
        got.append((lax.ppermute(chip_state, "y", pairs), lax.ppermute(chip_total, "y", pairs)))
    side_out = side(*side_inputs)
    got, side_out = lax.optimization_barrier((got, side_out))
    held = jnp.zeros_like(chip_state)
    gap = jnp.zeros_like(chip_total)
    for got_state, got_total in got:
        held = held + jnp.exp(gap)[:, None, None] * got_state
        gap = gap + got_total
    later = jnp.exp(early_total)[:, None, None] * held + early_state
    mine_in = jnp.where(first, held, later)
    other_in = swapped(jnp.where(first, later, held))
    return jnp.where(first, jnp.concatenate([mine_in, other_in]), jnp.concatenate([other_in, mine_in])), side_out


def pair_lanes(columns, pair):
    lane = lax.broadcasted_iota(jnp.int32, (columns.shape[0], 2 * HEAD_DIM), 1)
    return jnp.where(lane < HEAD_DIM, columns[:, 2 * pair : 2 * pair + 1], columns[:, 2 * pair + 1 : 2 * pair + 2])


def states_kernel(x_ref, b_ref, cum_ref, step_ref, out_ref):
    cum = cum_ref[0]
    weight = jnp.exp(cum[SPAN - 1 : SPAN, :] - cum) * step_ref[0]
    b_span = b_ref[...]
    for pair in range(GROUP // 2):
        lanes = slice(2 * HEAD_DIM * pair, 2 * HEAD_DIM * (pair + 1))
        decayed = (x_ref[:, lanes].astype(jnp.float32) * pair_lanes(weight, pair)).astype(jnp.bfloat16)
        out_ref[0, lanes, :] = lax.dot_general(
            decayed, b_span, (((0,), (0,)), ((), ())), preferred_element_type=jnp.float32
        )


def intra_kernel(x_ref, b_ref, c_ref, cum_ref, cum_row_ref, step_row_ref, gain_ref, part_ref):
    scores = lax.dot_general(c_ref[...], b_ref[...], (((1,), (1,)), ((), ())), preferred_element_type=jnp.float32)
    causal = lax.broadcasted_iota(jnp.int32, (SPAN, SPAN), 0) >= lax.broadcasted_iota(jnp.int32, (SPAN, SPAN), 1)
    cum = cum_ref[0]
    lane = lax.broadcasted_iota(jnp.int32, (SPAN, 2 * HEAD_DIM), 1)
    for pair in range(GROUP // 2):
        lanes = slice(2 * HEAD_DIM * pair, 2 * HEAD_DIM * (pair + 1))
        x_pair = x_ref[:, lanes]
        parts = []
        for half in range(2):
            head = 2 * pair + half
            spread = cum[:, head : head + 1] - cum_row_ref[head : head + 1, :]
            decay = jnp.where(causal, jnp.exp(jnp.where(causal, spread, 0.0)), 0.0)
            mixing = (scores * decay * step_row_ref[head : head + 1, :]).astype(jnp.bfloat16)
            parts.append(jnp.dot(mixing, x_pair, preferred_element_type=jnp.float32))
        intra = jnp.where(lane < HEAD_DIM, parts[0], parts[1])
        part_ref[:, lanes] = intra + gain_ref[:, lanes] * x_pair.astype(jnp.float32)


def readout_kernel(part_ref, c_ref, cum_ref, enter_ref, out_ref):
    rise = jnp.exp(cum_ref[0])
    c32 = c_ref[...].astype(jnp.float32)
    for pair in range(GROUP // 2):
        lanes = slice(2 * HEAD_DIM * pair, 2 * HEAD_DIM * (pair + 1))
        readout = lax.dot_general(
            c32, enter_ref[0, lanes, :], (((1,), (1,)), ((), ())),
            precision=lax.Precision.HIGHEST, preferred_element_type=jnp.float32,
        )
        out_ref[:, lanes] = (part_ref[:, lanes] + pair_lanes(rise, pair) * readout).astype(jnp.bfloat16)


def project(token_rows, input_weight):
    return lax.dot_general(
        token_rows,
        lax.all_gather(input_weight, ("dp",) + SEQ, axis=0, tiled=True),
        (((1,), (1,)), ((), ())),
        preferred_element_type=jnp.float32,
    ).astype(jnp.bfloat16)


def body(hidden, log_decay, input_weight, conv_weight, conv_bias, skip_gain):
    token_rows = hidden[0]
    length = token_rows.shape[0]
    span_count = length // SPAN
    groups = HALF_HEADS // GROUP
    projected = project(token_rows, input_weight)
    before_rows = shifted(projected[length - (CONV - 1) :], 1)
    extended = jnp.concatenate([before_rows, projected], axis=0)
    filtered = jnp.broadcast_to(conv_bias[None, :], (length, COLS))
    for kernel_tap in range(CONV):
        filtered = (
            filtered
            + extended[kernel_tap : kernel_tap + length].astype(jnp.float32)
            * conv_weight[kernel_tap].astype(jnp.float32)[None, :]
        )
    active = jax.nn.silu(filtered).astype(jnp.bfloat16)

    decay = log_decay[0]
    cum_row = jnp.cumsum(decay.reshape(HALF_HEADS, span_count, SPAN), axis=2).reshape(HALF_HEADS, length)
    step_row = -decay
    cum_grouped = cum_row.reshape(groups, GROUP, length).transpose(0, 2, 1)
    step_grouped = step_row.reshape(groups, GROUP, length).transpose(0, 2, 1)
    totals = cum_row.reshape(HALF_HEADS, span_count, SPAN)[:, :, -1].T

    x_spec = pl.BlockSpec((SPAN, GROUP * HEAD_DIM), lambda c, g: (c, g))
    b_spec = pl.BlockSpec((SPAN, STATE), lambda c, g: (c, INNER // STATE))
    c_spec = pl.BlockSpec((SPAN, STATE), lambda c, g: (c, INNER // STATE + 1))
    col_spec = pl.BlockSpec((1, SPAN, GROUP), lambda c, g: (g, c, 0))
    row_spec = pl.BlockSpec((GROUP, SPAN), lambda c, g: (g, c))
    state_spec = pl.BlockSpec((1, GROUP * HEAD_DIM, STATE), lambda c, g: (c, g, 0))
    gain = jnp.repeat(skip_gain, HEAD_DIM)[None, :]
    gain_spec = pl.BlockSpec((1, GROUP * HEAD_DIM), lambda c, g: (0, g))
    states = pl.pallas_call(
        states_kernel,
        grid=(span_count, groups),
        in_specs=[x_spec, b_spec, col_spec, col_spec],
        out_specs=state_spec,
        out_shape=jax.ShapeDtypeStruct((span_count, INNER, STATE), jnp.float32),
        cost_estimate=pl.CostEstimate(
            flops=2 * length * INNER * STATE, transcendentals=length * HALF_HEADS,
            bytes_accessed=2 * length * (INNER + STATE) + 4 * span_count * INNER * STATE,
        ),
    )(active, active, cum_grouped, step_grouped)
    states = states.reshape(span_count, HALF_HEADS, HEAD_DIM, STATE)

    local = jnp.zeros((HALF_HEADS, HEAD_DIM, STATE), jnp.float32)
    for span in range(span_count):
        local = jnp.exp(totals[span])[:, None, None] * local + states[span]
    def intra(active, cum_grouped, cum_row, step_row, gain):
        return pl.pallas_call(
            intra_kernel,
            grid=(span_count, groups),
            in_specs=[x_spec, b_spec, c_spec, col_spec, row_spec, row_spec, gain_spec],
            out_specs=x_spec,
            out_shape=jax.ShapeDtypeStruct((length, INNER), jnp.float32),
            cost_estimate=pl.CostEstimate(
                flops=2 * length * SPAN * (groups * STATE + 2 * INNER), transcendentals=length * SPAN * HALF_HEADS,
                bytes_accessed=2 * length * (INNER + 2 * STATE) + 4 * length * INNER,
            ),
        )(active, active, active, cum_grouped, cum_row, step_row, gain)

    held, part = scan_entering(
        jnp.sum(totals, axis=0), local, intra, (active, cum_grouped, cum_row, step_row, gain)
    )
    entering = []
    for span in range(span_count):
        entering.append(held)
        held = jnp.exp(totals[span])[:, None, None] * held + states[span]
    entering = jnp.stack(entering).reshape(span_count, INNER, STATE)

    out = pl.pallas_call(
        readout_kernel,
        grid=(span_count, groups),
        in_specs=[x_spec, c_spec, col_spec, state_spec],
        out_specs=x_spec,
        out_shape=jax.ShapeDtypeStruct((length, INNER), jnp.bfloat16),
        cost_estimate=pl.CostEstimate(
            flops=12 * length * STATE * INNER, transcendentals=length * HALF_HEADS,
            bytes_accessed=6 * length * INNER + 4 * span_count * INNER * STATE,
        ),
    )(part, active, cum_grouped, entering)
    return out[None]


def solution(mesh):
    split = Mesh(mesh.devices.reshape(mesh.shape["dp"], mesh.shape["seq"] // 2, 2), ("dp", "y", "core"))
    placed = (P("dp", SEQ, None), P("dp", None, SEQ), P(("dp",) + SEQ, None), P(), P(), P())
    return jax.shard_map(
        body, mesh=split, in_specs=placed, out_specs=P("dp", SEQ, None), check_vma=False
    )
```

```python
import jax
import jax.numpy as jnp
from jax import lax
from jax.experimental import pallas as pl
from jax.sharding import Mesh, PartitionSpec as P

HALF_HEADS = 40
HEAD_DIM = 64
STATE = 128
SPAN = 256
CONV = 4
INNER = 2560
COLS = 2816
GROUP = 8
SEQ = ("y", "core")


def shifted(array, by):
    peers = lax.axis_size(SEQ)
    pairs = [(i, i + by) for i in range(peers) if i + by < peers]
    return lax.ppermute(array, SEQ, pairs)


def swapped(array):
    return lax.ppermute(array, "core", [(0, 1), (1, 0)])


def scan_entering(total, state, side, side_inputs):
    core = lax.axis_index("core")
    half = HALF_HEADS // 2
    halves = state.reshape(STATE, 2, half, HEAD_DIM)
    mine = lax.dynamic_index_in_dim(halves, core, 1, False)
    sent = swapped(lax.dynamic_index_in_dim(halves, 1 - core, 1, False))
    totals = total.reshape(2, half)
    my_total = lax.dynamic_index_in_dim(totals, core, 0, False)
    peer_total = swapped(lax.dynamic_index_in_dim(totals, 1 - core, 0, False))
    first = core == 0
    early_state = jnp.where(first, mine, sent)
    late_state = jnp.where(first, sent, mine)
    early_total = jnp.where(first, my_total, peer_total)
    late_total = jnp.where(first, peer_total, my_total)
    chip_state = jnp.exp(late_total)[None, :, None] * early_state + late_state
    chip_total = early_total + late_total
    chips = lax.axis_size("y")
    chip_state, chip_total, side_inputs = lax.optimization_barrier((chip_state, chip_total, side_inputs))
    got = []
    for by in range(1, chips):
        pairs = [(i, i + by) for i in range(chips) if i + by < chips]
        got.append((lax.ppermute(chip_state, "y", pairs), lax.ppermute(chip_total, "y", pairs)))
    side_out = side(*side_inputs)
    got, side_out = lax.optimization_barrier((got, side_out))
    held = jnp.zeros_like(chip_state)
    gap = jnp.zeros_like(chip_total)
    for got_state, got_total in got:
        held = held + jnp.exp(gap)[None, :, None] * got_state
        gap = gap + got_total
    later = jnp.exp(early_total)[None, :, None] * held + early_state
    mine_in = jnp.where(first, held, later)
    other_in = swapped(jnp.where(first, later, held))
    joined = jnp.where(first, jnp.concatenate([mine_in, other_in], 1), jnp.concatenate([other_in, mine_in], 1))
    return joined, side_out


def pair_lanes(columns, pair):
    lane = lax.broadcasted_iota(jnp.int32, (columns.shape[0], 2 * HEAD_DIM), 1)
    return jnp.where(lane < HEAD_DIM, columns[:, 2 * pair : 2 * pair + 1], columns[:, 2 * pair + 1 : 2 * pair + 2])


def states_kernel(x_ref, bt_ref, cum_ref, step_ref, out_ref):
    cum = cum_ref[0]
    weight = jnp.exp(cum[SPAN - 1 : SPAN, :] - cum) * step_ref[0]
    b_flipped = bt_ref[...]
    for pair in range(GROUP // 2):
        lanes = slice(2 * HEAD_DIM * pair, 2 * HEAD_DIM * (pair + 1))
        decayed = (x_ref[:, lanes].astype(jnp.float32) * pair_lanes(weight, pair)).astype(jnp.bfloat16)
        out_ref[0, :, lanes] = jnp.dot(b_flipped, decayed, preferred_element_type=jnp.float32)


def intra_kernel(x_ref, b_ref, c_ref, cum_ref, cum_row_ref, step_row_ref, gain_ref, part_ref):
    scores = lax.dot_general(c_ref[...], b_ref[...], (((1,), (1,)), ((), ())), preferred_element_type=jnp.float32)
    causal = lax.broadcasted_iota(jnp.int32, (SPAN, SPAN), 0) >= lax.broadcasted_iota(jnp.int32, (SPAN, SPAN), 1)
    cum = cum_ref[0]
    lane = lax.broadcasted_iota(jnp.int32, (SPAN, 2 * HEAD_DIM), 1)
    for pair in range(GROUP // 2):
        lanes = slice(2 * HEAD_DIM * pair, 2 * HEAD_DIM * (pair + 1))
        x_pair = x_ref[:, lanes]
        parts = []
        for half in range(2):
            head = 2 * pair + half
            spread = cum[:, head : head + 1] - cum_row_ref[head : head + 1, :]
            decay = jnp.where(causal, jnp.exp(jnp.where(causal, spread, 0.0)), 0.0)
            mixing = (scores * decay * step_row_ref[head : head + 1, :]).astype(jnp.bfloat16)
            parts.append(jnp.dot(mixing, x_pair, preferred_element_type=jnp.float32))
        intra = jnp.where(lane < HEAD_DIM, parts[0], parts[1])
        part_ref[:, lanes] = intra + gain_ref[:, lanes] * x_pair.astype(jnp.float32)


def readout_kernel(part_ref, c_ref, cum_ref, enter_ref, out_ref):
    rise = jnp.exp(cum_ref[0])
    c32 = c_ref[...].astype(jnp.float32)
    for pair in range(GROUP // 2):
        lanes = slice(2 * HEAD_DIM * pair, 2 * HEAD_DIM * (pair + 1))
        readout = jnp.dot(
            c32, enter_ref[0, :, lanes], precision=lax.Precision.HIGHEST, preferred_element_type=jnp.float32
        )
        out_ref[:, lanes] = (part_ref[:, lanes] + pair_lanes(rise, pair) * readout).astype(jnp.bfloat16)


def project(token_rows, input_weight):
    return lax.dot_general(
        token_rows,
        lax.all_gather(input_weight, ("dp",) + SEQ, axis=0, tiled=True),
        (((1,), (1,)), ((), ())),
        preferred_element_type=jnp.float32,
    ).astype(jnp.bfloat16)


def body(hidden, log_decay, input_weight, conv_weight, conv_bias, skip_gain):
    token_rows = hidden[0]
    length = token_rows.shape[0]
    span_count = length // SPAN
    groups = HALF_HEADS // GROUP
    projected = project(token_rows, input_weight)
    before_rows = shifted(projected[length - (CONV - 1) :], 1)
    extended = jnp.concatenate([before_rows, projected], axis=0)
    filtered = jnp.broadcast_to(conv_bias[None, :], (length, COLS))
    for kernel_tap in range(CONV):
        filtered = (
            filtered
            + extended[kernel_tap : kernel_tap + length].astype(jnp.float32)
            * conv_weight[kernel_tap].astype(jnp.float32)[None, :]
        )
    active = jax.nn.silu(filtered).astype(jnp.bfloat16)

    decay = log_decay[0]
    cum_row = jnp.cumsum(decay.reshape(HALF_HEADS, span_count, SPAN), axis=2).reshape(HALF_HEADS, length)
    step_row = -decay
    cum_grouped = cum_row.reshape(groups, GROUP, length).transpose(0, 2, 1)
    step_grouped = step_row.reshape(groups, GROUP, length).transpose(0, 2, 1)
    totals = cum_row.reshape(HALF_HEADS, span_count, SPAN)[:, :, -1].T

    x_spec = pl.BlockSpec((SPAN, GROUP * HEAD_DIM), lambda c, g: (c, g))
    b_spec = pl.BlockSpec((SPAN, STATE), lambda c, g: (c, INNER // STATE))
    c_spec = pl.BlockSpec((SPAN, STATE), lambda c, g: (c, INNER // STATE + 1))
    col_spec = pl.BlockSpec((1, SPAN, GROUP), lambda c, g: (g, c, 0))
    row_spec = pl.BlockSpec((GROUP, SPAN), lambda c, g: (g, c))
    state_spec = pl.BlockSpec((1, STATE, GROUP * HEAD_DIM), lambda c, g: (c, 0, g))
    bt_spec = pl.BlockSpec((STATE, SPAN), lambda c, g: (0, c))
    b_flipped = active[:, INNER : INNER + STATE].T
    gain = jnp.repeat(skip_gain, HEAD_DIM)[None, :]
    gain_spec = pl.BlockSpec((1, GROUP * HEAD_DIM), lambda c, g: (0, g))
    states = pl.pallas_call(
        states_kernel,
        grid=(span_count, groups),
        in_specs=[x_spec, bt_spec, col_spec, col_spec],
        out_specs=state_spec,
        out_shape=jax.ShapeDtypeStruct((span_count, STATE, INNER), jnp.float32),
        cost_estimate=pl.CostEstimate(
            flops=2 * length * INNER * STATE, transcendentals=length * HALF_HEADS,
            bytes_accessed=2 * length * (INNER + STATE) + 4 * span_count * INNER * STATE,
        ),
    )(active, b_flipped, cum_grouped, step_grouped)
    states = states.reshape(span_count, STATE, HALF_HEADS, HEAD_DIM)

    local = jnp.zeros((STATE, HALF_HEADS, HEAD_DIM), jnp.float32)
    for span in range(span_count):
        local = jnp.exp(totals[span])[None, :, None] * local + states[span]
    def intra(active, cum_grouped, cum_row, step_row, gain):
        return pl.pallas_call(
            intra_kernel,
            grid=(span_count, groups),
            in_specs=[x_spec, b_spec, c_spec, col_spec, row_spec, row_spec, gain_spec],
            out_specs=x_spec,
            out_shape=jax.ShapeDtypeStruct((length, INNER), jnp.float32),
            cost_estimate=pl.CostEstimate(
                flops=2 * length * SPAN * (groups * STATE + 2 * INNER), transcendentals=length * SPAN * HALF_HEADS,
                bytes_accessed=2 * length * (INNER + 2 * STATE) + 4 * length * INNER,
            ),
        )(active, active, active, cum_grouped, cum_row, step_row, gain)

    held, part = scan_entering(
        jnp.sum(totals, axis=0), local, intra, (active, cum_grouped, cum_row, step_row, gain)
    )
    entering = []
    for span in range(span_count):
        entering.append(held)
        held = jnp.exp(totals[span])[None, :, None] * held + states[span]
    entering = jnp.stack(entering).reshape(span_count, STATE, INNER)

    out = pl.pallas_call(
        readout_kernel,
        grid=(span_count, groups),
        in_specs=[x_spec, c_spec, col_spec, state_spec],
        out_specs=x_spec,
        out_shape=jax.ShapeDtypeStruct((length, INNER), jnp.bfloat16),
        cost_estimate=pl.CostEstimate(
            flops=12 * length * STATE * INNER, transcendentals=length * HALF_HEADS,
            bytes_accessed=6 * length * INNER + 4 * span_count * INNER * STATE,
        ),
    )(part, active, cum_grouped, entering)
    return out[None]


def solution(mesh):
    split = Mesh(mesh.devices.reshape(mesh.shape["dp"], mesh.shape["seq"] // 2, 2), ("dp", "y", "core"))
    placed = (P("dp", SEQ, None), P("dp", None, SEQ), P(("dp",) + SEQ, None), P(), P(), P())
    return jax.shard_map(
        body, mesh=split, in_specs=placed, out_specs=P("dp", SEQ, None), check_vma=False
    )
```

```python
import jax
import jax.numpy as jnp
from jax import lax
from jax.experimental import pallas as pl
from jax.sharding import Mesh, PartitionSpec as P

HALF_HEADS = 40
HEAD_DIM = 64
STATE = 128
SPAN = 256
CONV = 4
INNER = 2560
COLS = 2816
GROUP = 8
SEQ = ("y", "core")


def shifted(array, by):
    peers = lax.axis_size(SEQ)
    pairs = [(i, i + by) for i in range(peers) if i + by < peers]
    return lax.ppermute(array, SEQ, pairs)


def swapped(array):
    return lax.ppermute(array, "core", [(0, 1), (1, 0)])


def with_total(state, total):
    row = jnp.broadcast_to(total[:, None, None], (state.shape[0], 1, state.shape[2]))
    return jnp.concatenate([state, row], axis=1)


def scan_entering(total, state, side, side_inputs):
    core = lax.axis_index("core")
    half = HALF_HEADS // 2
    halves = state.reshape(2, half, HEAD_DIM, STATE)
    totals = total.reshape(2, half)
    mine = lax.dynamic_index_in_dim(halves, core, 0, False)
    my_total = lax.dynamic_index_in_dim(totals, core, 0, False)
    packed = swapped(
        with_total(
            lax.dynamic_index_in_dim(halves, 1 - core, 0, False),
            lax.dynamic_index_in_dim(totals, 1 - core, 0, False),
        )
    )
    sent, peer_total = packed[:, :HEAD_DIM], packed[:, HEAD_DIM, 0]
    first = core == 0
    early_state = jnp.where(first, mine, sent)
    late_state = jnp.where(first, sent, mine)
    early_total = jnp.where(first, my_total, peer_total)
    late_total = jnp.where(first, peer_total, my_total)
    chip_state = jnp.exp(late_total)[:, None, None] * early_state + late_state
    chip_total = early_total + late_total
    chips = lax.axis_size("y")
    chip_packed, side_inputs = lax.optimization_barrier((with_total(chip_state, chip_total), side_inputs))
    got = []
    for by in range(1, chips):
        pairs = [(i, i + by) for i in range(chips) if i + by < chips]
        got.append(lax.ppermute(chip_packed, "y", pairs))
    side_out = side(*side_inputs)
    got, side_out = lax.optimization_barrier((got, side_out))
    held = jnp.zeros_like(chip_state)
    gap = jnp.zeros_like(chip_total)
    for got_packed in got:
        held = held + jnp.exp(gap)[:, None, None] * got_packed[:, :HEAD_DIM]
        gap = gap + got_packed[:, HEAD_DIM, 0]
    later = jnp.exp(early_total)[:, None, None] * held + early_state
    mine_in = jnp.where(first, held, later)
    other_in = swapped(jnp.where(first, later, held))
    joined = jnp.where(first, jnp.concatenate([mine_in, other_in]), jnp.concatenate([other_in, mine_in]))
    return joined, side_out


def pair_lanes(columns, pair):
    lane = lax.broadcasted_iota(jnp.int32, (columns.shape[0], 2 * HEAD_DIM), 1)
    return jnp.where(lane < HEAD_DIM, columns[:, 2 * pair : 2 * pair + 1], columns[:, 2 * pair + 1 : 2 * pair + 2])


def states_kernel(x_ref, b_ref, cum_ref, step_ref, out_ref):
    cum = cum_ref[0]
    weight = jnp.exp(cum[SPAN - 1 : SPAN, :] - cum) * step_ref[0]
    b_span = b_ref[...]
    for pair in range(GROUP // 2):
        lanes = slice(2 * HEAD_DIM * pair, 2 * HEAD_DIM * (pair + 1))
        decayed = (x_ref[:, lanes].astype(jnp.float32) * pair_lanes(weight, pair)).astype(jnp.bfloat16)
        out_ref[0, lanes, :] = lax.dot_general(
            decayed, b_span, (((0,), (0,)), ((), ())), preferred_element_type=jnp.float32
        )


def intra_kernel(x_ref, b_ref, c_ref, cum_ref, cum_row_ref, step_row_ref, gain_ref, part_ref):
    scores = lax.dot_general(c_ref[...], b_ref[...], (((1,), (1,)), ((), ())), preferred_element_type=jnp.float32)
    causal = lax.broadcasted_iota(jnp.int32, (SPAN, SPAN), 0) >= lax.broadcasted_iota(jnp.int32, (SPAN, SPAN), 1)
    cum = cum_ref[0]
    lane = lax.broadcasted_iota(jnp.int32, (SPAN, 2 * HEAD_DIM), 1)
    for pair in range(GROUP // 2):
        lanes = slice(2 * HEAD_DIM * pair, 2 * HEAD_DIM * (pair + 1))
        x_pair = x_ref[:, lanes]
        parts = []
        for half in range(2):
            head = 2 * pair + half
            spread = cum[:, head : head + 1] - cum_row_ref[head : head + 1, :]
            decay = jnp.where(causal, jnp.exp(jnp.where(causal, spread, 0.0)), 0.0)
            mixing = (scores * decay * step_row_ref[head : head + 1, :]).astype(jnp.bfloat16)
            parts.append(jnp.dot(mixing, x_pair, preferred_element_type=jnp.float32))
        intra = jnp.where(lane < HEAD_DIM, parts[0], parts[1])
        part_ref[:, lanes] = intra + gain_ref[:, lanes] * x_pair.astype(jnp.float32)


def readout_kernel(part_ref, c_ref, cum_ref, enter_ref, out_ref):
    rise = jnp.exp(cum_ref[0])
    c32 = c_ref[...].astype(jnp.float32)
    for pair in range(GROUP // 2):
        lanes = slice(2 * HEAD_DIM * pair, 2 * HEAD_DIM * (pair + 1))
        readout = lax.dot_general(
            c32, enter_ref[0, lanes, :], (((1,), (1,)), ((), ())),
            precision=lax.Precision.HIGHEST, preferred_element_type=jnp.float32,
        )
        out_ref[:, lanes] = (part_ref[:, lanes] + pair_lanes(rise, pair) * readout).astype(jnp.bfloat16)


def project(token_rows, input_weight):
    return lax.dot_general(
        token_rows,
        lax.all_gather(input_weight, ("dp",) + SEQ, axis=0, tiled=True),
        (((1,), (1,)), ((), ())),
        preferred_element_type=jnp.float32,
    ).astype(jnp.bfloat16)


def body(hidden, log_decay, input_weight, conv_weight, conv_bias, skip_gain):
    token_rows = hidden[0]
    length = token_rows.shape[0]
    span_count = length // SPAN
    groups = HALF_HEADS // GROUP
    projected = project(token_rows, input_weight)
    before_rows = shifted(projected[length - (CONV - 1) :], 1)
    extended = jnp.concatenate([before_rows, projected], axis=0)
    filtered = jnp.broadcast_to(conv_bias[None, :], (length, COLS))
    for kernel_tap in range(CONV):
        filtered = (
            filtered
            + extended[kernel_tap : kernel_tap + length].astype(jnp.float32)
            * conv_weight[kernel_tap].astype(jnp.float32)[None, :]
        )
    active = jax.nn.silu(filtered).astype(jnp.bfloat16)

    decay = log_decay[0]
    cum_row = jnp.cumsum(decay.reshape(HALF_HEADS, span_count, SPAN), axis=2).reshape(HALF_HEADS, length)
    step_row = -decay
    cum_grouped = cum_row.reshape(groups, GROUP, length).transpose(0, 2, 1)
    step_grouped = step_row.reshape(groups, GROUP, length).transpose(0, 2, 1)
    totals = cum_row.reshape(HALF_HEADS, span_count, SPAN)[:, :, -1].T

    x_spec = pl.BlockSpec((SPAN, GROUP * HEAD_DIM), lambda c, g: (c, g))
    b_spec = pl.BlockSpec((SPAN, STATE), lambda c, g: (c, INNER // STATE))
    c_spec = pl.BlockSpec((SPAN, STATE), lambda c, g: (c, INNER // STATE + 1))
    col_spec = pl.BlockSpec((1, SPAN, GROUP), lambda c, g: (g, c, 0))
    row_spec = pl.BlockSpec((GROUP, SPAN), lambda c, g: (g, c))
    state_spec = pl.BlockSpec((1, GROUP * HEAD_DIM, STATE), lambda c, g: (c, g, 0))
    gain = jnp.repeat(skip_gain, HEAD_DIM)[None, :]
    gain_spec = pl.BlockSpec((1, GROUP * HEAD_DIM), lambda c, g: (0, g))
    states = pl.pallas_call(
        states_kernel,
        grid=(span_count, groups),
        in_specs=[x_spec, b_spec, col_spec, col_spec],
        out_specs=state_spec,
        out_shape=jax.ShapeDtypeStruct((span_count, INNER, STATE), jnp.float32),
        cost_estimate=pl.CostEstimate(
            flops=2 * length * INNER * STATE, transcendentals=length * HALF_HEADS,
            bytes_accessed=2 * length * (INNER + STATE) + 4 * span_count * INNER * STATE,
        ),
    )(active, active, cum_grouped, step_grouped)
    states = states.reshape(span_count, HALF_HEADS, HEAD_DIM, STATE)

    local = jnp.zeros((HALF_HEADS, HEAD_DIM, STATE), jnp.float32)
    for span in range(span_count):
        local = jnp.exp(totals[span])[:, None, None] * local + states[span]
    def intra(active, cum_grouped, cum_row, step_row, gain):
        return pl.pallas_call(
            intra_kernel,
            grid=(span_count, groups),
            in_specs=[x_spec, b_spec, c_spec, col_spec, row_spec, row_spec, gain_spec],
            out_specs=x_spec,
            out_shape=jax.ShapeDtypeStruct((length, INNER), jnp.float32),
            cost_estimate=pl.CostEstimate(
                flops=2 * length * SPAN * (groups * STATE + 2 * INNER), transcendentals=length * SPAN * HALF_HEADS,
                bytes_accessed=2 * length * (INNER + 2 * STATE) + 4 * length * INNER,
            ),
        )(active, active, active, cum_grouped, cum_row, step_row, gain)

    held, part = scan_entering(
        jnp.sum(totals, axis=0), local, intra, (active, cum_grouped, cum_row, step_row, gain)
    )
    entering = []
    for span in range(span_count):
        entering.append(held)
        held = jnp.exp(totals[span])[:, None, None] * held + states[span]
    entering = jnp.stack(entering).reshape(span_count, INNER, STATE)

    out = pl.pallas_call(
        readout_kernel,
        grid=(span_count, groups),
        in_specs=[x_spec, c_spec, col_spec, state_spec],
        out_specs=x_spec,
        out_shape=jax.ShapeDtypeStruct((length, INNER), jnp.bfloat16),
        cost_estimate=pl.CostEstimate(
            flops=12 * length * STATE * INNER, transcendentals=length * HALF_HEADS,
            bytes_accessed=6 * length * INNER + 4 * span_count * INNER * STATE,
        ),
    )(part, active, cum_grouped, entering)
    return out[None]


def solution(mesh):
    split = Mesh(mesh.devices.reshape(mesh.shape["dp"], mesh.shape["seq"] // 2, 2), ("dp", "y", "core"))
    placed = (P("dp", SEQ, None), P("dp", None, SEQ), P(("dp",) + SEQ, None), P(), P(), P())
    return jax.shard_map(
        body, mesh=split, in_specs=placed, out_specs=P("dp", SEQ, None), check_vma=False
    )
```

```python
import jax
import jax.numpy as jnp
from jax import lax
from jax.experimental import pallas as pl
from jax.sharding import Mesh, PartitionSpec as P

HALF_HEADS = 40
HEAD_DIM = 64
STATE = 128
SPAN = 256
CONV = 4
INNER = 2560
COLS = 2816
GROUP = 8
SEQ = ("y", "core")


def shifted(array, by):
    peers = lax.axis_size(SEQ)
    pairs = [(i, i + by) for i in range(peers) if i + by < peers]
    return lax.ppermute(array, SEQ, pairs)


def swapped(array):
    return lax.ppermute(array, "core", [(0, 1), (1, 0)])


def scan_entering(total, state, side, side_inputs):
    core = lax.axis_index("core")
    half = HALF_HEADS // 2
    halves = state.reshape(2, half, HEAD_DIM, STATE)
    mine = lax.dynamic_index_in_dim(halves, core, 0, False)
    sent = swapped(lax.dynamic_index_in_dim(halves, 1 - core, 0, False))
    totals = total.reshape(2, half)
    my_total = lax.dynamic_index_in_dim(totals, core, 0, False)
    peer_total = swapped(lax.dynamic_index_in_dim(totals, 1 - core, 0, False))
    first = core == 0
    early_state = jnp.where(first, mine, sent)
    late_state = jnp.where(first, sent, mine)
    early_total = jnp.where(first, my_total, peer_total)
    late_total = jnp.where(first, peer_total, my_total)
    chip_state = jnp.exp(late_total)[:, None, None] * early_state + late_state
    chip_total = early_total + late_total
    chips = lax.axis_size("y")
    chip_state, chip_total, side_inputs = lax.optimization_barrier((chip_state, chip_total, side_inputs))
    got = []
    for by in range(1, chips):
        pairs = [(i, i + by) for i in range(chips) if i + by < chips]
        got.append((lax.ppermute(chip_state, "y", pairs), lax.ppermute(chip_total, "y", pairs)))
    side_out = side(*side_inputs)
    got, side_out = lax.optimization_barrier((got, side_out))
    held = jnp.zeros_like(chip_state)
    gap = jnp.zeros_like(chip_total)
    for got_state, got_total in got:
        held = held + jnp.exp(gap)[:, None, None] * got_state
        gap = gap + got_total
    later = jnp.exp(early_total)[:, None, None] * held + early_state
    mine_in = jnp.where(first, held, later)
    other_in = swapped(jnp.where(first, later, held))
    return jnp.where(first, jnp.concatenate([mine_in, other_in]), jnp.concatenate([other_in, mine_in])), side_out


def pair_lanes(columns, pair):
    lane = lax.broadcasted_iota(jnp.int32, (columns.shape[0], 2 * HEAD_DIM), 1)
    return jnp.where(lane < HEAD_DIM, columns[:, 2 * pair : 2 * pair + 1], columns[:, 2 * pair + 1 : 2 * pair + 2])


def states_kernel(x_ref, b_ref, cum_ref, step_ref, out_ref):
    cum = cum_ref[0]
    weight = jnp.exp(cum[SPAN - 1 : SPAN, :] - cum) * step_ref[0]
    b_span = b_ref[...]
    for pair in range(GROUP // 2):
        lanes = slice(2 * HEAD_DIM * pair, 2 * HEAD_DIM * (pair + 1))
        decayed = (x_ref[:, lanes].astype(jnp.float32) * pair_lanes(weight, pair)).astype(jnp.bfloat16)
        out_ref[0, lanes, :] = lax.dot_general(
            decayed, b_span, (((0,), (0,)), ((), ())), preferred_element_type=jnp.float32
        )


def intra_kernel(x_ref, b_ref, c_ref, cum_ref, cum_row_ref, step_row_ref, gain_ref, part_ref):
    scores = lax.dot_general(c_ref[...], b_ref[...], (((1,), (1,)), ((), ())), preferred_element_type=jnp.float32)
    causal = lax.broadcasted_iota(jnp.int32, (SPAN, SPAN), 0) >= lax.broadcasted_iota(jnp.int32, (SPAN, SPAN), 1)
    cum = cum_ref[0]
    lane = lax.broadcasted_iota(jnp.int32, (SPAN, 2 * HEAD_DIM), 1)
    for pair in range(GROUP // 2):
        lanes = slice(2 * HEAD_DIM * pair, 2 * HEAD_DIM * (pair + 1))
        x_pair = x_ref[:, lanes]
        parts = []
        for half in range(2):
            head = 2 * pair + half
            spread = cum[:, head : head + 1] - cum_row_ref[head : head + 1, :]
            decay = jnp.where(causal, jnp.exp(jnp.where(causal, spread, 0.0)), 0.0)
            mixing = (scores * decay * step_row_ref[head : head + 1, :]).astype(jnp.bfloat16)
            parts.append(jnp.dot(mixing, x_pair, preferred_element_type=jnp.float32))
        intra = jnp.where(lane < HEAD_DIM, parts[0], parts[1])
        part_ref[:, lanes] = intra + gain_ref[:, lanes] * x_pair.astype(jnp.float32)


def readout_kernel(part_ref, c_ref, cum_ref, enter_ref, out_ref):
    rise = jnp.exp(cum_ref[0])
    c32 = c_ref[...].astype(jnp.float32)
    for pair in range(GROUP // 2):
        lanes = slice(2 * HEAD_DIM * pair, 2 * HEAD_DIM * (pair + 1))
        readout = lax.dot_general(
            c32, enter_ref[0, lanes, :], (((1,), (1,)), ((), ())),
            precision=lax.Precision.HIGH, preferred_element_type=jnp.float32,
        )
        out_ref[:, lanes] = (part_ref[:, lanes] + pair_lanes(rise, pair) * readout).astype(jnp.bfloat16)


def project(token_rows, input_weight):
    return lax.dot_general(
        token_rows,
        lax.all_gather(input_weight, ("dp",) + SEQ, axis=0, tiled=True),
        (((1,), (1,)), ((), ())),
        preferred_element_type=jnp.float32,
    ).astype(jnp.bfloat16)


def body(hidden, log_decay, input_weight, conv_weight, conv_bias, skip_gain):
    token_rows = hidden[0]
    length = token_rows.shape[0]
    span_count = length // SPAN
    groups = HALF_HEADS // GROUP
    projected = project(token_rows, input_weight)
    before_rows = shifted(projected[length - (CONV - 1) :], 1)
    extended = jnp.concatenate([before_rows, projected], axis=0)
    filtered = jnp.broadcast_to(conv_bias[None, :], (length, COLS))
    for kernel_tap in range(CONV):
        filtered = (
            filtered
            + extended[kernel_tap : kernel_tap + length].astype(jnp.float32)
            * conv_weight[kernel_tap].astype(jnp.float32)[None, :]
        )
    active = jax.nn.silu(filtered).astype(jnp.bfloat16)

    decay = log_decay[0]
    cum_row = jnp.cumsum(decay.reshape(HALF_HEADS, span_count, SPAN), axis=2).reshape(HALF_HEADS, length)
    step_row = -decay
    cum_grouped = cum_row.reshape(groups, GROUP, length).transpose(0, 2, 1)
    step_grouped = step_row.reshape(groups, GROUP, length).transpose(0, 2, 1)
    totals = cum_row.reshape(HALF_HEADS, span_count, SPAN)[:, :, -1].T

    x_spec = pl.BlockSpec((SPAN, GROUP * HEAD_DIM), lambda c, g: (c, g))
    b_spec = pl.BlockSpec((SPAN, STATE), lambda c, g: (c, INNER // STATE))
    c_spec = pl.BlockSpec((SPAN, STATE), lambda c, g: (c, INNER // STATE + 1))
    col_spec = pl.BlockSpec((1, SPAN, GROUP), lambda c, g: (g, c, 0))
    row_spec = pl.BlockSpec((GROUP, SPAN), lambda c, g: (g, c))
    state_spec = pl.BlockSpec((1, GROUP * HEAD_DIM, STATE), lambda c, g: (c, g, 0))
    gain = jnp.repeat(skip_gain, HEAD_DIM)[None, :]
    gain_spec = pl.BlockSpec((1, GROUP * HEAD_DIM), lambda c, g: (0, g))
    states = pl.pallas_call(
        states_kernel,
        grid=(span_count, groups),
        in_specs=[x_spec, b_spec, col_spec, col_spec],
        out_specs=state_spec,
        out_shape=jax.ShapeDtypeStruct((span_count, INNER, STATE), jnp.float32),
        cost_estimate=pl.CostEstimate(
            flops=2 * length * INNER * STATE, transcendentals=length * HALF_HEADS,
            bytes_accessed=2 * length * (INNER + STATE) + 4 * span_count * INNER * STATE,
        ),
    )(active, active, cum_grouped, step_grouped)
    states = states.reshape(span_count, HALF_HEADS, HEAD_DIM, STATE)

    local = jnp.zeros((HALF_HEADS, HEAD_DIM, STATE), jnp.float32)
    for span in range(span_count):
        local = jnp.exp(totals[span])[:, None, None] * local + states[span]
    def intra(active, cum_grouped, cum_row, step_row, gain):
        return pl.pallas_call(
            intra_kernel,
            grid=(span_count, groups),
            in_specs=[x_spec, b_spec, c_spec, col_spec, row_spec, row_spec, gain_spec],
            out_specs=x_spec,
            out_shape=jax.ShapeDtypeStruct((length, INNER), jnp.float32),
            cost_estimate=pl.CostEstimate(
                flops=2 * length * SPAN * (groups * STATE + 2 * INNER), transcendentals=length * SPAN * HALF_HEADS,
                bytes_accessed=2 * length * (INNER + 2 * STATE) + 4 * length * INNER,
            ),
        )(active, active, active, cum_grouped, cum_row, step_row, gain)

    held, part = scan_entering(
        jnp.sum(totals, axis=0), local, intra, (active, cum_grouped, cum_row, step_row, gain)
    )
    entering = []
    for span in range(span_count):
        entering.append(held)
        held = jnp.exp(totals[span])[:, None, None] * held + states[span]
    entering = jnp.stack(entering).reshape(span_count, INNER, STATE)

    out = pl.pallas_call(
        readout_kernel,
        grid=(span_count, groups),
        in_specs=[x_spec, c_spec, col_spec, state_spec],
        out_specs=x_spec,
        out_shape=jax.ShapeDtypeStruct((length, INNER), jnp.bfloat16),
        cost_estimate=pl.CostEstimate(
            flops=12 * length * STATE * INNER, transcendentals=length * HALF_HEADS,
            bytes_accessed=6 * length * INNER + 4 * span_count * INNER * STATE,
        ),
    )(part, active, cum_grouped, entering)
    return out[None]


def solution(mesh):
    split = Mesh(mesh.devices.reshape(mesh.shape["dp"], mesh.shape["seq"] // 2, 2), ("dp", "y", "core"))
    placed = (P("dp", SEQ, None), P("dp", None, SEQ), P(("dp",) + SEQ, None), P(), P(), P())
    return jax.shard_map(
        body, mesh=split, in_specs=placed, out_specs=P("dp", SEQ, None), check_vma=False
    )
```

```python
import jax
import jax.numpy as jnp
from jax import lax
from jax.experimental import pallas as pl
from jax.sharding import Mesh, PartitionSpec as P

HALF_HEADS = 40
HEAD_DIM = 64
STATE = 128
SPAN = 256
CONV = 4
INNER = 2560
COLS = 2816
GROUP = 40
SEQ = ("y", "core")


def shifted(array, by):
    peers = lax.axis_size(SEQ)
    pairs = [(i, i + by) for i in range(peers) if i + by < peers]
    return lax.ppermute(array, SEQ, pairs)


def swapped(array):
    return lax.ppermute(array, "core", [(0, 1), (1, 0)])


def scan_entering(total, state, side, side_inputs):
    core = lax.axis_index("core")
    half = HALF_HEADS // 2
    halves = state.reshape(2, half, HEAD_DIM, STATE)
    mine = lax.dynamic_index_in_dim(halves, core, 0, False)
    sent = swapped(lax.dynamic_index_in_dim(halves, 1 - core, 0, False))
    totals = total.reshape(2, half)
    my_total = lax.dynamic_index_in_dim(totals, core, 0, False)
    peer_total = swapped(lax.dynamic_index_in_dim(totals, 1 - core, 0, False))
    first = core == 0
    early_state = jnp.where(first, mine, sent)
    late_state = jnp.where(first, sent, mine)
    early_total = jnp.where(first, my_total, peer_total)
    late_total = jnp.where(first, peer_total, my_total)
    chip_state = jnp.exp(late_total)[:, None, None] * early_state + late_state
    chip_total = early_total + late_total
    chips = lax.axis_size("y")
    chip_state, chip_total, side_inputs = lax.optimization_barrier((chip_state, chip_total, side_inputs))
    got = []
    for by in range(1, chips):
        pairs = [(i, i + by) for i in range(chips) if i + by < chips]
        got.append((lax.ppermute(chip_state, "y", pairs), lax.ppermute(chip_total, "y", pairs)))
    side_out = side(*side_inputs)
    got, side_out = lax.optimization_barrier((got, side_out))
    held = jnp.zeros_like(chip_state)
    gap = jnp.zeros_like(chip_total)
    for got_state, got_total in got:
        held = held + jnp.exp(gap)[:, None, None] * got_state
        gap = gap + got_total
    later = jnp.exp(early_total)[:, None, None] * held + early_state
    mine_in = jnp.where(first, held, later)
    other_in = swapped(jnp.where(first, later, held))
    return jnp.where(first, jnp.concatenate([mine_in, other_in]), jnp.concatenate([other_in, mine_in])), side_out


def pair_lanes(columns, pair):
    lane = lax.broadcasted_iota(jnp.int32, (columns.shape[0], 2 * HEAD_DIM), 1)
    return jnp.where(lane < HEAD_DIM, columns[:, 2 * pair : 2 * pair + 1], columns[:, 2 * pair + 1 : 2 * pair + 2])


def states_kernel(x_ref, b_ref, cum_ref, step_ref, out_ref):
    cum = cum_ref[0]
    weight = jnp.exp(cum[SPAN - 1 : SPAN, :] - cum) * step_ref[0]
    b_span = b_ref[...]
    for pair in range(GROUP // 2):
        lanes = slice(2 * HEAD_DIM * pair, 2 * HEAD_DIM * (pair + 1))
        decayed = (x_ref[:, lanes].astype(jnp.float32) * pair_lanes(weight, pair)).astype(jnp.bfloat16)
        out_ref[0, lanes, :] = lax.dot_general(
            decayed, b_span, (((0,), (0,)), ((), ())), preferred_element_type=jnp.float32
        )


def intra_kernel(x_ref, b_ref, c_ref, cum_ref, cum_row_ref, step_row_ref, gain_ref, part_ref):
    scores = lax.dot_general(c_ref[...], b_ref[...], (((1,), (1,)), ((), ())), preferred_element_type=jnp.float32)
    causal = lax.broadcasted_iota(jnp.int32, (SPAN, SPAN), 0) >= lax.broadcasted_iota(jnp.int32, (SPAN, SPAN), 1)
    cum = cum_ref[0]
    lane = lax.broadcasted_iota(jnp.int32, (SPAN, 2 * HEAD_DIM), 1)
    for pair in range(GROUP // 2):
        lanes = slice(2 * HEAD_DIM * pair, 2 * HEAD_DIM * (pair + 1))
        x_pair = x_ref[:, lanes]
        parts = []
        for half in range(2):
            head = 2 * pair + half
            spread = cum[:, head : head + 1] - cum_row_ref[head : head + 1, :]
            decay = jnp.where(causal, jnp.exp(jnp.where(causal, spread, 0.0)), 0.0)
            mixing = (scores * decay * step_row_ref[head : head + 1, :]).astype(jnp.bfloat16)
            parts.append(jnp.dot(mixing, x_pair, preferred_element_type=jnp.float32))
        intra = jnp.where(lane < HEAD_DIM, parts[0], parts[1])
        part_ref[:, lanes] = intra + gain_ref[:, lanes] * x_pair.astype(jnp.float32)


def readout_kernel(part_ref, c_ref, cum_ref, enter_ref, out_ref):
    rise = jnp.exp(cum_ref[0])
    c32 = c_ref[...].astype(jnp.float32)
    for pair in range(GROUP // 2):
        lanes = slice(2 * HEAD_DIM * pair, 2 * HEAD_DIM * (pair + 1))
        readout = lax.dot_general(
            c32, enter_ref[0, lanes, :], (((1,), (1,)), ((), ())),
            precision=lax.Precision.HIGH, preferred_element_type=jnp.float32,
        )
        out_ref[:, lanes] = (part_ref[:, lanes] + pair_lanes(rise, pair) * readout).astype(jnp.bfloat16)


def project(token_rows, input_weight):
    return lax.dot_general(
        token_rows,
        lax.all_gather(input_weight, ("dp",) + SEQ, axis=0, tiled=True),
        (((1,), (1,)), ((), ())),
        preferred_element_type=jnp.float32,
    ).astype(jnp.bfloat16)


def body(hidden, log_decay, input_weight, conv_weight, conv_bias, skip_gain):
    token_rows = hidden[0]
    length = token_rows.shape[0]
    span_count = length // SPAN
    groups = HALF_HEADS // GROUP
    projected = project(token_rows, input_weight)
    before_rows = shifted(projected[length - (CONV - 1) :], 1)
    extended = jnp.concatenate([before_rows, projected], axis=0)
    filtered = jnp.broadcast_to(conv_bias[None, :], (length, COLS))
    for kernel_tap in range(CONV):
        filtered = (
            filtered
            + extended[kernel_tap : kernel_tap + length].astype(jnp.float32)
            * conv_weight[kernel_tap].astype(jnp.float32)[None, :]
        )
    active = jax.nn.silu(filtered).astype(jnp.bfloat16)

    decay = log_decay[0]
    cum_row = jnp.cumsum(decay.reshape(HALF_HEADS, span_count, SPAN), axis=2).reshape(HALF_HEADS, length)
    step_row = -decay
    cum_grouped = cum_row.reshape(groups, GROUP, length).transpose(0, 2, 1)
    step_grouped = step_row.reshape(groups, GROUP, length).transpose(0, 2, 1)
    totals = cum_row.reshape(HALF_HEADS, span_count, SPAN)[:, :, -1].T

    x_spec = pl.BlockSpec((SPAN, GROUP * HEAD_DIM), lambda c, g: (c, g))
    b_spec = pl.BlockSpec((SPAN, STATE), lambda c, g: (c, INNER // STATE))
    c_spec = pl.BlockSpec((SPAN, STATE), lambda c, g: (c, INNER // STATE + 1))
    col_spec = pl.BlockSpec((1, SPAN, GROUP), lambda c, g: (g, c, 0))
    row_spec = pl.BlockSpec((GROUP, SPAN), lambda c, g: (g, c))
    state_spec = pl.BlockSpec((1, GROUP * HEAD_DIM, STATE), lambda c, g: (c, g, 0))
    gain = jnp.repeat(skip_gain, HEAD_DIM)[None, :]
    gain_spec = pl.BlockSpec((1, GROUP * HEAD_DIM), lambda c, g: (0, g))
    states = pl.pallas_call(
        states_kernel,
        grid=(span_count, groups),
        in_specs=[x_spec, b_spec, col_spec, col_spec],
        out_specs=state_spec,
        out_shape=jax.ShapeDtypeStruct((span_count, INNER, STATE), jnp.float32),
        cost_estimate=pl.CostEstimate(
            flops=2 * length * INNER * STATE, transcendentals=length * HALF_HEADS,
            bytes_accessed=2 * length * (INNER + STATE) + 4 * span_count * INNER * STATE,
        ),
    )(active, active, cum_grouped, step_grouped)
    states = states.reshape(span_count, HALF_HEADS, HEAD_DIM, STATE)

    local = jnp.zeros((HALF_HEADS, HEAD_DIM, STATE), jnp.float32)
    for span in range(span_count):
        local = jnp.exp(totals[span])[:, None, None] * local + states[span]
    def intra(active, cum_grouped, cum_row, step_row, gain):
        return pl.pallas_call(
            intra_kernel,
            grid=(span_count, groups),
            in_specs=[x_spec, b_spec, c_spec, col_spec, row_spec, row_spec, gain_spec],
            out_specs=x_spec,
            out_shape=jax.ShapeDtypeStruct((length, INNER), jnp.float32),
            cost_estimate=pl.CostEstimate(
                flops=2 * length * SPAN * (groups * STATE + 2 * INNER), transcendentals=length * SPAN * HALF_HEADS,
                bytes_accessed=2 * length * (INNER + 2 * STATE) + 4 * length * INNER,
            ),
        )(active, active, active, cum_grouped, cum_row, step_row, gain)

    held, part = scan_entering(
        jnp.sum(totals, axis=0), local, intra, (active, cum_grouped, cum_row, step_row, gain)
    )
    entering = []
    for span in range(span_count):
        entering.append(held)
        held = jnp.exp(totals[span])[:, None, None] * held + states[span]
    entering = jnp.stack(entering).reshape(span_count, INNER, STATE)

    out = pl.pallas_call(
        readout_kernel,
        grid=(span_count, groups),
        in_specs=[x_spec, c_spec, col_spec, state_spec],
        out_specs=x_spec,
        out_shape=jax.ShapeDtypeStruct((length, INNER), jnp.bfloat16),
        cost_estimate=pl.CostEstimate(
            flops=12 * length * STATE * INNER, transcendentals=length * HALF_HEADS,
            bytes_accessed=6 * length * INNER + 4 * span_count * INNER * STATE,
        ),
    )(part, active, cum_grouped, entering)
    return out[None]


def solution(mesh):
    split = Mesh(mesh.devices.reshape(mesh.shape["dp"], mesh.shape["seq"] // 2, 2), ("dp", "y", "core"))
    placed = (P("dp", SEQ, None), P("dp", None, SEQ), P(("dp",) + SEQ, None), P(), P(), P())
    return jax.shard_map(
        body, mesh=split, in_specs=placed, out_specs=P("dp", SEQ, None), check_vma=False
    )
```

```python
import jax
import jax.numpy as jnp
from jax import lax
from jax.experimental import pallas as pl
from jax.sharding import Mesh, PartitionSpec as P

HALF_HEADS = 40
HEAD_DIM = 64
STATE = 128
SPAN = 256
CONV = 4
INNER = 2560
COLS = 2816
GROUP = 40
SEQ = ("y", "core")


def shifted(array, by):
    peers = lax.axis_size(SEQ)
    pairs = [(i, i + by) for i in range(peers) if i + by < peers]
    return lax.ppermute(array, SEQ, pairs)


def swapped(array):
    return lax.ppermute(array, "core", [(0, 1), (1, 0)])


def scan_entering(total, state, side, side_inputs):
    core = lax.axis_index("core")
    half = HALF_HEADS // 2
    halves = state.reshape(2, half, HEAD_DIM, STATE)
    mine = lax.dynamic_index_in_dim(halves, core, 0, False)
    sent = swapped(lax.dynamic_index_in_dim(halves, 1 - core, 0, False))
    totals = total.reshape(2, half)
    my_total = lax.dynamic_index_in_dim(totals, core, 0, False)
    peer_total = swapped(lax.dynamic_index_in_dim(totals, 1 - core, 0, False))
    first = core == 0
    early_state = jnp.where(first, mine, sent)
    late_state = jnp.where(first, sent, mine)
    early_total = jnp.where(first, my_total, peer_total)
    late_total = jnp.where(first, peer_total, my_total)
    chip_state = jnp.exp(late_total)[:, None, None] * early_state + late_state
    chip_total = early_total + late_total
    chips = lax.axis_size("y")
    chip_state, chip_total, side_inputs = lax.optimization_barrier((chip_state, chip_total, side_inputs))
    got = []
    for by in range(1, chips):
        pairs = [(i, i + by) for i in range(chips) if i + by < chips]
        got.append((lax.ppermute(chip_state, "y", pairs), lax.ppermute(chip_total, "y", pairs)))
    side_out = side(*side_inputs)
    got, side_out = lax.optimization_barrier((got, side_out))
    held = jnp.zeros_like(chip_state)
    gap = jnp.zeros_like(chip_total)
    for got_state, got_total in got:
        held = held + jnp.exp(gap)[:, None, None] * got_state
        gap = gap + got_total
    later = jnp.exp(early_total)[:, None, None] * held + early_state
    mine_in = jnp.where(first, held, later)
    other_in = swapped(jnp.where(first, later, held))
    return jnp.where(first, jnp.concatenate([mine_in, other_in]), jnp.concatenate([other_in, mine_in])), side_out


def pair_lanes(columns, pair):
    lane = lax.broadcasted_iota(jnp.int32, (columns.shape[0], 2 * HEAD_DIM), 1)
    return jnp.where(lane < HEAD_DIM, columns[:, 2 * pair : 2 * pair + 1], columns[:, 2 * pair + 1 : 2 * pair + 2])


def states_kernel(x_ref, b_ref, cum_ref, step_ref, out_ref):
    cum = cum_ref[0]
    weight = jnp.exp(cum[SPAN - 1 : SPAN, :] - cum) * step_ref[0]
    b_span = b_ref[...]
    for pair in range(GROUP // 2):
        lanes = slice(2 * HEAD_DIM * pair, 2 * HEAD_DIM * (pair + 1))
        decayed = (x_ref[:, lanes].astype(jnp.float32) * pair_lanes(weight, pair)).astype(jnp.bfloat16)
        out_ref[0, lanes, :] = lax.dot_general(
            decayed, b_span, (((0,), (0,)), ((), ())), preferred_element_type=jnp.float32
        )


def intra_kernel(x_ref, b_ref, c_ref, cum_ref, cum_row_ref, step_row_ref, gain_ref, part_ref):
    scores = lax.dot_general(c_ref[...], b_ref[...], (((1,), (1,)), ((), ())), preferred_element_type=jnp.float32)
    causal = lax.broadcasted_iota(jnp.int32, (SPAN, SPAN), 0) >= lax.broadcasted_iota(jnp.int32, (SPAN, SPAN), 1)
    cum = cum_ref[0]
    lane = lax.broadcasted_iota(jnp.int32, (SPAN, 2 * HEAD_DIM), 1)
    for pair in range(GROUP // 2):
        lanes = slice(2 * HEAD_DIM * pair, 2 * HEAD_DIM * (pair + 1))
        x_pair = x_ref[:, lanes]
        parts = []
        for half in range(2):
            head = 2 * pair + half
            spread = cum[:, head : head + 1] - cum_row_ref[head : head + 1, :]
            decay = jnp.exp(jnp.where(causal, spread, -jnp.inf))
            mixing = (scores * decay * step_row_ref[head : head + 1, :]).astype(jnp.bfloat16)
            parts.append(jnp.dot(mixing, x_pair, preferred_element_type=jnp.float32))
        intra = jnp.where(lane < HEAD_DIM, parts[0], parts[1])
        part_ref[:, lanes] = intra + gain_ref[:, lanes] * x_pair.astype(jnp.float32)


def readout_kernel(part_ref, c_ref, cum_ref, enter_ref, out_ref):
    rise = jnp.exp(cum_ref[0])
    c32 = c_ref[...].astype(jnp.float32)
    for pair in range(GROUP // 2):
        lanes = slice(2 * HEAD_DIM * pair, 2 * HEAD_DIM * (pair + 1))
        readout = lax.dot_general(
            c32, enter_ref[0, lanes, :], (((1,), (1,)), ((), ())),
            precision=lax.Precision.HIGH, preferred_element_type=jnp.float32,
        )
        out_ref[:, lanes] = (part_ref[:, lanes] + pair_lanes(rise, pair) * readout).astype(jnp.bfloat16)


def project(token_rows, input_weight):
    return lax.dot_general(
        token_rows,
        lax.all_gather(input_weight, ("dp",) + SEQ, axis=0, tiled=True),
        (((1,), (1,)), ((), ())),
        preferred_element_type=jnp.float32,
    ).astype(jnp.bfloat16)


def body(hidden, log_decay, input_weight, conv_weight, conv_bias, skip_gain):
    token_rows = hidden[0]
    length = token_rows.shape[0]
    span_count = length // SPAN
    groups = HALF_HEADS // GROUP
    projected = project(token_rows, input_weight)
    before_rows = shifted(projected[length - (CONV - 1) :], 1)
    extended = jnp.concatenate([before_rows, projected], axis=0)
    filtered = jnp.broadcast_to(conv_bias[None, :], (length, COLS))
    for kernel_tap in range(CONV):
        filtered = (
            filtered
            + extended[kernel_tap : kernel_tap + length].astype(jnp.float32)
            * conv_weight[kernel_tap].astype(jnp.float32)[None, :]
        )
    active = jax.nn.silu(filtered).astype(jnp.bfloat16)

    decay = log_decay[0]
    cum_row = jnp.cumsum(decay.reshape(HALF_HEADS, span_count, SPAN), axis=2).reshape(HALF_HEADS, length)
    step_row = -decay
    cum_grouped = cum_row.reshape(groups, GROUP, length).transpose(0, 2, 1)
    step_grouped = step_row.reshape(groups, GROUP, length).transpose(0, 2, 1)
    totals = cum_row.reshape(HALF_HEADS, span_count, SPAN)[:, :, -1].T

    x_spec = pl.BlockSpec((SPAN, GROUP * HEAD_DIM), lambda c, g: (c, g))
    b_spec = pl.BlockSpec((SPAN, STATE), lambda c, g: (c, INNER // STATE))
    c_spec = pl.BlockSpec((SPAN, STATE), lambda c, g: (c, INNER // STATE + 1))
    col_spec = pl.BlockSpec((1, SPAN, GROUP), lambda c, g: (g, c, 0))
    row_spec = pl.BlockSpec((GROUP, SPAN), lambda c, g: (g, c))
    state_spec = pl.BlockSpec((1, GROUP * HEAD_DIM, STATE), lambda c, g: (c, g, 0))
    gain = jnp.repeat(skip_gain, HEAD_DIM)[None, :]
    gain_spec = pl.BlockSpec((1, GROUP * HEAD_DIM), lambda c, g: (0, g))
    states = pl.pallas_call(
        states_kernel,
        grid=(span_count, groups),
        in_specs=[x_spec, b_spec, col_spec, col_spec],
        out_specs=state_spec,
        out_shape=jax.ShapeDtypeStruct((span_count, INNER, STATE), jnp.float32),
        cost_estimate=pl.CostEstimate(
            flops=2 * length * INNER * STATE, transcendentals=length * HALF_HEADS,
            bytes_accessed=2 * length * (INNER + STATE) + 4 * span_count * INNER * STATE,
        ),
    )(active, active, cum_grouped, step_grouped)
    states = states.reshape(span_count, HALF_HEADS, HEAD_DIM, STATE)

    local = jnp.zeros((HALF_HEADS, HEAD_DIM, STATE), jnp.float32)
    for span in range(span_count):
        local = jnp.exp(totals[span])[:, None, None] * local + states[span]
    def intra(active, cum_grouped, cum_row, step_row, gain):
        return pl.pallas_call(
            intra_kernel,
            grid=(span_count, groups),
            in_specs=[x_spec, b_spec, c_spec, col_spec, row_spec, row_spec, gain_spec],
            out_specs=x_spec,
            out_shape=jax.ShapeDtypeStruct((length, INNER), jnp.float32),
            cost_estimate=pl.CostEstimate(
                flops=2 * length * SPAN * (groups * STATE + 2 * INNER), transcendentals=length * SPAN * HALF_HEADS,
                bytes_accessed=2 * length * (INNER + 2 * STATE) + 4 * length * INNER,
            ),
        )(active, active, active, cum_grouped, cum_row, step_row, gain)

    held, part = scan_entering(
        jnp.sum(totals, axis=0), local, intra, (active, cum_grouped, cum_row, step_row, gain)
    )
    entering = []
    for span in range(span_count):
        entering.append(held)
        held = jnp.exp(totals[span])[:, None, None] * held + states[span]
    entering = jnp.stack(entering).reshape(span_count, INNER, STATE)

    out = pl.pallas_call(
        readout_kernel,
        grid=(span_count, groups),
        in_specs=[x_spec, c_spec, col_spec, state_spec],
        out_specs=x_spec,
        out_shape=jax.ShapeDtypeStruct((length, INNER), jnp.bfloat16),
        cost_estimate=pl.CostEstimate(
            flops=12 * length * STATE * INNER, transcendentals=length * HALF_HEADS,
            bytes_accessed=6 * length * INNER + 4 * span_count * INNER * STATE,
        ),
    )(part, active, cum_grouped, entering)
    return out[None]


def solution(mesh):
    split = Mesh(mesh.devices.reshape(mesh.shape["dp"], mesh.shape["seq"] // 2, 2), ("dp", "y", "core"))
    placed = (P("dp", SEQ, None), P("dp", None, SEQ), P(("dp",) + SEQ, None), P(), P(), P())
    return jax.shard_map(
        body, mesh=split, in_specs=placed, out_specs=P("dp", SEQ, None), check_vma=False
    )
```
